1024 devices in a mesh: group: 64 (over z_lo, x, core), section: 16 (over y, z_hi).
Axes of the slice: x: 4, y: 4, z: 32 (z_hi: 4, z_lo: 8; z = z_hi * 8 + z_lo), core: 2. Of those that a mesh axis runs over, the one named last changes fastest.
Arguments:
- proj_rows: bfloat16 [16, 8192, 2560], P('section', 'group')
- out_grad: bfloat16 [16, 8192, 2048], P('section', 'group'), may hold values from -6 to 6
- prefix_kv: bfloat16 [16, 512, 512], P('section', 'group'), may hold values from -6 to 6
- prefix_len: int32 [8], replicated, may hold values from 1 to 192, 512 in all
- comp_len: int32 [64], replicated, may hold values from 1 to 128, as said below
- owner: int32 [64], replicated, may hold values from 0 to 7, as said below
Outputs:
- passed_grad: bfloat16 [16, 8192, 2048], P('section', 'group')
- comp_kv_grad: bfloat16 [16, 8192, 512], P('section', 'group')
- prefix_grad: bfloat16 [16, 512, 512], P('section', 'group')
The draws below stay inside these ranges and needn't reach their ends.
Inputs may be any that keep to these rules, and one draw needn't show every extreme that they name: `owner`: each prompt has exactly 8 completions. `comp_len`: some completion has length exactly 128. `prefix_len`: the lengths sum to 512.
All inputs are finite; a program needn't handle non-finite values.
Results may differ from the reference program's by a relative error of at most 0.012.
Values may be sent and summed in bfloat16 or wider, within the bound.
No kernel may reach another device: no remote copies, remote signals or barrier semaphores. Data moves between devices by JAX's collectives and lax.ppermute only.
A program may use at most 32 MiB of HBM per device.

```python
import math
import jax
import jax.numpy as jnp
import numpy as np
from jax import lax

HEADS = 16
KV_HEADS = 2
HEAD_DIM = 128
CPP = 8
CTOK = 128
SECTIONS = 16
COMPS = 64
ROWS = 8192
PROMPTS = 8
PSLOTS = 512
PMOST = 192


def draw_proj_rows(key, part):
    first = jax.random.fold_in(key, 0)
    width = HEADS * HEAD_DIM
    kv_width = KV_HEADS * HEAD_DIM
    shape = (SECTIONS, ROWS, width + 2 * kv_width)
    base = jax.random.normal(first, shape, jnp.float32)
    queries = base[..., :width]
    keys = base[..., width:width + kv_width]
    values = base[..., width + kv_width:]
    return jnp.concatenate([queries, keys, values], axis=-1).astype(jnp.bfloat16)


def draw_comp_len(key, part):
    first, second = jax.random.split(key, 2)
    lengths = jax.random.randint(first, (COMPS,), max(CTOK // 4, 1), CTOK + 1)
    chosen = jax.random.randint(second, (), 0, COMPS)
    return jnp.where(jnp.arange(COMPS) == chosen, CTOK, lengths).astype(jnp.int32)


def draw_owner(key, part):
    return jax.random.permutation(key, jnp.arange(COMPS) // CPP).astype(jnp.int32)


def shard_levels(own_key, extent, cuts, low, high):
    gain, own = 1.0, jax.random.fold_in(own_key, 6)
    for axis_at, parts in cuts:
        draws = jnp.exp(jax.random.uniform(jax.random.fold_in(own, axis_at), (parts,), jnp.float32, low / len(cuts), high / len(cuts)))
        gain = gain * jnp.repeat(draws, extent[axis_at] // parts).reshape([-1 if axis == axis_at else 1 for axis in range(len(extent))])
    return gain


def split_up(amount, total, limit, slope):
    weights = [(1 << 20) // math.isqrt(grade ** slope) + 1 for grade in range(2, amount + 1)]
    rest, counts = total - limit - (amount - 1), [1] * (amount - 1)
    while rest > 0:
        free = [i for i in range(amount - 1) if counts[i] < limit]
        whole, budget = sum([weights[i] for i in free]), rest
        for i in free:
            addition = min(limit - counts[i], max(1, budget * weights[i] // whole), rest)
            counts[i] = counts[i] + addition
            rest = rest - addition
    return np.array([limit] + counts)


def uneven_parts(stream_key, amount, total, limit, skew):
    if amount == 2:
        one = jax.random.randint(stream_key, (), max(1, total - limit), min(limit, total - 1) + 1)
        return jnp.stack([one, total - one])
    sizes = jnp.asarray(split_up(amount, total, limit, skew), jnp.int32)
    couples = (amount - 1) // 2
    donor, receiver = sizes[1:1 + 2 * couples:2], sizes[2:2 + 2 * couples:2]
    margin = jnp.minimum(donor - 1, limit - receiver)
    shifted = jax.random.randint(jax.random.fold_in(stream_key, 1), (couples,), 0, 1 << 20) % (margin + 1)
    sizes = sizes.at[1:1 + 2 * couples:2].set(donor - shifted).at[2:2 + 2 * couples:2].set(receiver + shifted)
    return sizes[jax.random.permutation(jax.random.fold_in(stream_key, 2), amount)]


def bell_draw(stream_key, shape, scale, reach, pieces=(), held_as=jnp.bfloat16):
    array = scale * jax.random.normal(stream_key, shape, jnp.float32)
    if pieces:
        array = array * shard_levels(stream_key, shape, pieces, -0.22, 0.18)
    return jnp.clip(array, -reach, reach).astype(held_as)


def setup_inputs(seed: int = 0) -> dict:
    key_of = jax.random.split(jax.random.key(seed), 7)
    proj_rows = draw_proj_rows(jax.random.fold_in(key_of[6], 71), 0)
    out_grad = bell_draw(key_of[1], (SECTIONS, ROWS, HEADS * HEAD_DIM), 1.0, 6.0, ((0, 16), (1, 64)))
    prefix_kv = bell_draw(key_of[2], (SECTIONS, PSLOTS, 2 * KV_HEADS * HEAD_DIM), 1.0, 6.0, ((0, 16), (1, 64)))
    prefix_len = uneven_parts(key_of[3], PROMPTS, PSLOTS, PMOST, 2).astype(jnp.int32)
    comp_len = draw_comp_len(jax.random.fold_in(key_of[6], 71), 0)
    owner = draw_owner(jax.random.fold_in(key_of[6], 71), 0)
    return {"proj_rows": proj_rows, "out_grad": out_grad, "prefix_kv": prefix_kv, "prefix_len": prefix_len, "comp_len": comp_len, "owner": owner}


def attend_back(queries, keys, values, dout, allowed):
    count = queries.shape[0]
    total = keys.shape[0]
    per = HEADS // KV_HEADS
    scale = HEAD_DIM ** -0.5
    q_four = queries.reshape(count, KV_HEADS, per, HEAD_DIM).astype(jnp.float32)
    d_four = dout.reshape(count, KV_HEADS, per, HEAD_DIM).astype(jnp.float32)
    k_three = keys.reshape(total, KV_HEADS, HEAD_DIM).astype(jnp.float32)
    v_three = values.reshape(total, KV_HEADS, HEAD_DIM).astype(jnp.float32)
    scores = jnp.einsum("rgqh,mgh->gqrm", q_four, k_three) * scale
    scores = jnp.where(allowed[None, None], scores, jnp.float32(-1e30))
    top = jnp.max(scores, axis=-1, keepdims=True)
    expo = jnp.exp(scores - top)
    weights = expo / jnp.sum(expo, axis=-1, keepdims=True)
    w_low = lax.optimization_barrier(weights.astype(jnp.bfloat16))
    w_back = w_low.astype(jnp.float32)
    output = jnp.einsum("gqrm,mgh->gqrh", w_back, v_three)
    delta = jnp.einsum("rgqh,gqrh->gqr", d_four, output)
    dprob = jnp.einsum("rgqh,mgh->gqrm", d_four, v_three)
    d_low = lax.optimization_barrier((weights * (dprob - delta[..., None])).astype(jnp.bfloat16))
    d_back = d_low.astype(jnp.float32)
    grad_q = (jnp.einsum("gqrm,mgh->rgqh", d_back, k_three) * scale).reshape(count, HEADS * HEAD_DIM)
    grad_k = (jnp.einsum("gqrm,rgqh->mgh", d_back, q_four) * scale).reshape(total, KV_HEADS * HEAD_DIM)
    grad_v = jnp.einsum("gqrm,rgqh->mgh", w_back, d_four).reshape(total, KV_HEADS * HEAD_DIM)
    return grad_q.astype(jnp.bfloat16), grad_k, grad_v


def reference(proj_rows, out_grad, prefix_kv, prefix_len, comp_len, owner):
    width = HEADS * HEAD_DIM
    kv_width = KV_HEADS * HEAD_DIM
    starts = jnp.cumsum(prefix_len) - prefix_len
    slot_ids = jnp.arange(PSLOTS)
    token_ids = jnp.arange(CTOK)
    causal = token_ids[:, None] >= token_ids[None, :]

    def one_section(section_args):
        rows_s, grad_s, prefix_s = section_args
        rows_c = rows_s.reshape(COMPS, CTOK, width + 2 * kv_width)
        grad_c = grad_s.reshape(COMPS, CTOK, width)

        def step(total, item):
            rows, grad, prompt, length = item
            offset = starts[prompt]
            span = prefix_len[prompt]
            inside = (slot_ids >= offset) & (slot_ids < offset + span)
            live = token_ids < length
            dout = jnp.where(live[:, None], grad, jnp.zeros_like(grad))
            keys = jnp.concatenate([prefix_s[:, :kv_width], rows[:, width:width + kv_width]], axis=0)
            values = jnp.concatenate([prefix_s[:, kv_width:], rows[:, width + kv_width:]], axis=0)
            allowed = jnp.concatenate([jnp.broadcast_to(inside[None, :], (CTOK, PSLOTS)), causal], axis=1)
            grad_q, grad_k, grad_v = attend_back(rows[:, :width], keys, values, dout, allowed)
            prefix_term = jnp.concatenate([grad_k[:PSLOTS], grad_v[:PSLOTS]], axis=1)
            own = jnp.concatenate([grad_k[PSLOTS:], grad_v[PSLOTS:]], axis=1).astype(jnp.bfloat16)
            return total + prefix_term, (grad_q, own)

        init = jnp.zeros((PSLOTS, 2 * kv_width), jnp.float32)
        total, (grad_q, own) = lax.scan(step, init, (rows_c, grad_c, owner, comp_len))
        return grad_q.reshape(ROWS, width), own.reshape(ROWS, 2 * kv_width), total.astype(jnp.bfloat16)

    grad_q, own, prefix_grad = lax.map(one_section, (proj_rows, out_grad, prefix_kv))
    passed = jnp.concatenate([grad_q[1:], grad_q[:1]], axis=0)
    return passed, own, prefix_grad
```

```python
import jax
import jax.numpy as jnp
from jax import lax
from jax.sharding import PartitionSpec as P

HEADS = 16
KV_HEADS = 2
HEAD_DIM = 128


def from_behind(value, axis, steps):
    count = lax.axis_size(axis)
    pairs = [(source, (source + steps) % count) for source in range(count)]
    return lax.ppermute(value, axis, pairs)


def score_block(q_four, keys):
    total = keys.shape[0]
    k_three = keys.reshape(total, KV_HEADS, HEAD_DIM)
    return jnp.einsum(
        "rgqh,mgh->gqrm", q_four, k_three, preferred_element_type=jnp.float32
    ) * HEAD_DIM ** (-0.5)


def key_terms(d_low, w_low, q_four, d_four, total):
    grad_k = jnp.einsum(
        "gqrm,rgqh->mgh", d_low, q_four, preferred_element_type=jnp.float32
    ) * HEAD_DIM ** (-0.5)
    grad_v = jnp.einsum("gqrm,rgqh->mgh", w_low, d_four, preferred_element_type=jnp.float32)
    return (grad_k.reshape(total, KV_HEADS * HEAD_DIM), grad_v.reshape(total, KV_HEADS * HEAD_DIM))


def per_device(proj_rows, out_grad, prefix_kv, prefix_len, comp_len, owner):
    width = HEADS * HEAD_DIM
    kv_width = KV_HEADS * HEAD_DIM
    per = HEADS // KV_HEADS
    rows = proj_rows[0]
    count = rows.shape[0]
    queries = rows[:, :width]
    own_keys = rows[:, width : width + kv_width]
    own_values = rows[:, width + kv_width :]
    member = lax.axis_index("group")
    groups = lax.axis_size("group")
    picked = jnp.arange(groups) == member
    prompt = jnp.sum(jnp.where(picked, owner, 0))
    length = jnp.sum(jnp.where(picked, comp_len, 0))
    prompt_count = prefix_len.shape[0]
    prompt_ids = jnp.arange(prompt_count)
    offset = jnp.sum(jnp.where(prompt_ids < prompt, prefix_len, 0))
    span = jnp.sum(jnp.where(prompt_ids == prompt, prefix_len, 0))
    token_ids = jnp.arange(count)
    live = token_ids < length
    dout = jnp.where(live[:, None], out_grad[0], jnp.zeros_like(out_grad[0]))
    block = prefix_kv[0]
    spread = jnp.broadcast_to(block[None], (groups,) + block.shape)
    gathered = lax.all_to_all(spread, "group", 0, 0, tiled=True)
    gathered = gathered.reshape(groups * block.shape[0], block.shape[1])
    slots = gathered.shape[0]
    window = min(slots, 3 * slots // prompt_count)
    first = jnp.minimum(offset, slots - window)
    window_rows = lax.dynamic_slice_in_dim(gathered, first, window, 0)
    positions = first + jnp.arange(window)
    inside = (positions >= offset) & (positions < offset + span)
    causal = token_ids[:, None] >= token_ids[None, :]
    keys = jnp.concatenate([window_rows[:, :kv_width], own_keys], axis=0)
    values = jnp.concatenate([window_rows[:, kv_width:], own_values], axis=0)
    allowed = jnp.concatenate([jnp.broadcast_to(inside[None, :], (count, window)), causal], axis=1)
    total_keys = window + count
    q_four = queries.reshape(count, KV_HEADS, per, HEAD_DIM)
    d_four = dout.reshape(count, KV_HEADS, per, HEAD_DIM)
    v_three = values.reshape(total_keys, KV_HEADS, HEAD_DIM)
    scores = jnp.where(allowed[None, None], score_block(q_four, keys), jnp.float32(-1e30))
    top = jnp.max(scores, axis=-1, keepdims=True)
    expo = jnp.exp(scores - top)
    denom = jnp.sum(expo, axis=-1, keepdims=True)
    weights = expo / denom
    w_low = weights.astype(jnp.bfloat16)
    output = jnp.einsum("gqrm,mgh->gqrh", w_low, v_three, preferred_element_type=jnp.float32)
    delta = jnp.einsum("rgqh,gqrh->gqr", d_four.astype(jnp.float32), output)
    dprob = jnp.einsum("rgqh,mgh->gqrm", d_four, v_three, preferred_element_type=jnp.float32)
    d_low = (weights * (dprob - delta[..., None])).astype(jnp.bfloat16)
    k_three = keys.reshape(total_keys, KV_HEADS, HEAD_DIM)
    grad_q = jnp.einsum(
        "gqrm,mgh->rgqh", d_low, k_three, preferred_element_type=jnp.float32
    ) * HEAD_DIM ** (-0.5)
    grad_q = grad_q.reshape(count, width).astype(jnp.bfloat16)
    grad_own_k, grad_own_v = key_terms(
        d_low[..., window:], w_low[..., window:], q_four, d_four, count
    )
    own_grad = jnp.concatenate([grad_own_k, grad_own_v], axis=1).astype(jnp.bfloat16)
    passed = from_behind(grad_q[None], "section", -1)
    grad_pk, grad_pv = key_terms(d_low[..., :window], w_low[..., :window], q_four, d_four, window)
    window_term = jnp.concatenate([grad_pk, grad_pv], axis=1)
    full_term = lax.dynamic_update_slice_in_dim(
        jnp.zeros((slots, 2 * kv_width), jnp.float32), window_term, first, 0
    )
    pieces = full_term.reshape(groups, slots // groups, 2 * kv_width)
    prefix_grad = lax.all_to_all(pieces, "group", 0, 0, tiled=True).sum(axis=0)
    return (passed, own_grad[None], prefix_grad.astype(jnp.bfloat16)[None])


def solution(mesh):
    in_specs = (
        P("section", "group", None),
        P("section", "group", None),
        P("section", "group", None),
        P(),
        P(),
        P(),
    )
    out_specs = (
        P("section", "group", None),
        P("section", "group", None),
        P("section", "group", None),
    )
    return jax.shard_map(
        per_device, mesh=mesh, in_specs=in_specs, out_specs=out_specs, check_vma=False
    )
```

```python
import jax
import jax.numpy as jnp
from jax import lax
from jax.sharding import Mesh, PartitionSpec as P

HEADS = 16
KV_HEADS = 2
HEAD_DIM = 128

FAR = "group_z"
NEAR = ("group_x", "group_core")
GROUP = (FAR,) + NEAR
SECTION = ("section_y", "section_z")


def gather_prefix(block):
    far = lax.axis_size(FAR)
    near = lax.axis_size(NEAR)
    rows, width = block.shape
    spread = jnp.broadcast_to(block[None], (far, rows, width))
    column = lax.all_to_all(spread, FAR, 0, 0, tiled=True).reshape(far * rows, width)
    spread = jnp.broadcast_to(column[None], (near, far * rows, width))
    whole = lax.all_to_all(spread, NEAR, 0, 0, tiled=True)
    whole = whole.reshape(near, far, rows, width).transpose(1, 0, 2, 3)
    return whole.reshape(far * near * rows, width)


def scatter_sum(term):
    far = lax.axis_size(FAR)
    near = lax.axis_size(NEAR)
    slots, width = term.shape
    rows = slots // (far * near)
    parts = term.reshape(far, near, rows, width).transpose(1, 0, 2, 3)
    parts = lax.all_to_all(parts, NEAR, 0, 0, tiled=True).sum(axis=0)
    return lax.all_to_all(parts, FAR, 0, 0, tiled=True).sum(axis=0)


def from_behind(value, axis, steps):
    count = lax.axis_size(axis)
    pairs = [(source, (source + steps) % count) for source in range(count)]
    return lax.ppermute(value, axis, pairs)


def score_block(q_four, keys):
    total = keys.shape[0]
    k_three = keys.reshape(total, KV_HEADS, HEAD_DIM)
    return jnp.einsum(
        "rgqh,mgh->gqrm", q_four, k_three, preferred_element_type=jnp.float32
    ) * HEAD_DIM ** (-0.5)


def key_terms(d_low, w_low, q_four, d_four, total):
    grad_k = jnp.einsum(
        "gqrm,rgqh->mgh", d_low, q_four, preferred_element_type=jnp.float32
    ) * HEAD_DIM ** (-0.5)
    grad_v = jnp.einsum("gqrm,rgqh->mgh", w_low, d_four, preferred_element_type=jnp.float32)
    return (grad_k.reshape(total, KV_HEADS * HEAD_DIM), grad_v.reshape(total, KV_HEADS * HEAD_DIM))


def per_device(proj_rows, out_grad, prefix_kv, prefix_len, comp_len, owner):
    width = HEADS * HEAD_DIM
    kv_width = KV_HEADS * HEAD_DIM
    per = HEADS // KV_HEADS
    rows = proj_rows[0]
    count = rows.shape[0]
    queries = rows[:, :width]
    own_keys = rows[:, width : width + kv_width]
    own_values = rows[:, width + kv_width :]
    member = (lax.axis_index(FAR) * lax.axis_size(NEAR[0]) + lax.axis_index(NEAR[0])) * lax.axis_size(
        NEAR[1]
    ) + lax.axis_index(NEAR[1])
    groups = lax.axis_size(FAR) * lax.axis_size(NEAR)
    picked = jnp.arange(groups) == member
    prompt = jnp.sum(jnp.where(picked, owner, 0))
    length = jnp.sum(jnp.where(picked, comp_len, 0))
    prompt_count = prefix_len.shape[0]
    prompt_ids = jnp.arange(prompt_count)
    offset = jnp.sum(jnp.where(prompt_ids < prompt, prefix_len, 0))
    span = jnp.sum(jnp.where(prompt_ids == prompt, prefix_len, 0))
    token_ids = jnp.arange(count)
    live = token_ids < length
    dout = jnp.where(live[:, None], out_grad[0], jnp.zeros_like(out_grad[0]))
    gathered = gather_prefix(prefix_kv[0])
    slots = gathered.shape[0]
    window = min(slots, 3 * slots // prompt_count)
    first = jnp.minimum(offset, slots - window)
    window_rows = lax.dynamic_slice_in_dim(gathered, first, window, 0)
    positions = first + jnp.arange(window)
    inside = (positions >= offset) & (positions < offset + span)
    causal = token_ids[:, None] >= token_ids[None, :]
    keys = jnp.concatenate([window_rows[:, :kv_width], own_keys], axis=0)
    values = jnp.concatenate([window_rows[:, kv_width:], own_values], axis=0)
    allowed = jnp.concatenate([jnp.broadcast_to(inside[None, :], (count, window)), causal], axis=1)
    total_keys = window + count
    q_four = queries.reshape(count, KV_HEADS, per, HEAD_DIM)
    d_four = dout.reshape(count, KV_HEADS, per, HEAD_DIM)
    v_three = values.reshape(total_keys, KV_HEADS, HEAD_DIM)
    scores = jnp.where(allowed[None, None], score_block(q_four, keys), jnp.float32(-1e30))
    top = jnp.max(scores, axis=-1, keepdims=True)
    expo = jnp.exp(scores - top)
    denom = jnp.sum(expo, axis=-1, keepdims=True)
    weights = expo / denom
    w_low = weights.astype(jnp.bfloat16)
    output = jnp.einsum("gqrm,mgh->gqrh", w_low, v_three, preferred_element_type=jnp.float32)
    delta = jnp.einsum("rgqh,gqrh->gqr", d_four.astype(jnp.float32), output)
    dprob = jnp.einsum("rgqh,mgh->gqrm", d_four, v_three, preferred_element_type=jnp.float32)
    d_low = (weights * (dprob - delta[..., None])).astype(jnp.bfloat16)
    k_three = keys.reshape(total_keys, KV_HEADS, HEAD_DIM)
    grad_q = jnp.einsum(
        "gqrm,mgh->rgqh", d_low, k_three, preferred_element_type=jnp.float32
    ) * HEAD_DIM ** (-0.5)
    grad_q = grad_q.reshape(count, width).astype(jnp.bfloat16)
    grad_own_k, grad_own_v = key_terms(
        d_low[..., window:], w_low[..., window:], q_four, d_four, count
    )
    own_grad = jnp.concatenate([grad_own_k, grad_own_v], axis=1).astype(jnp.bfloat16)
    passed = from_behind(grad_q[None], SECTION, -1)
    grad_pk, grad_pv = key_terms(d_low[..., :window], w_low[..., :window], q_four, d_four, window)
    window_term = jnp.concatenate([grad_pk, grad_pv], axis=1)
    full_term = lax.dynamic_update_slice_in_dim(
        jnp.zeros((slots, 2 * kv_width), jnp.float32), window_term, first, 0
    )
    prefix_grad = scatter_sum(full_term)
    return (passed, own_grad[None], prefix_grad.astype(jnp.bfloat16)[None])


def solution(mesh):
    group_size = mesh.shape["group"]
    section_size = mesh.shape["section"]
    near_x, near_core = 4, 2
    layout = mesh.devices.reshape(
        group_size // (near_x * near_core), near_x, near_core, section_size // 4, 4
    )
    split = Mesh(layout, GROUP + SECTION)
    placed = P(SECTION, GROUP, None)
    in_specs = (placed, placed, placed, P(), P(), P())
    out_specs = (placed, placed, placed)
    return jax.shard_map(
        per_device, mesh=split, in_specs=in_specs, out_specs=out_specs, check_vma=False
    )
```

```python
import jax
import jax.numpy as jnp
from jax import lax
from jax.sharding import Mesh, PartitionSpec as P

HEADS = 16
KV_HEADS = 2
HEAD_DIM = 128

FAR = "group_z"
NEAR = ("group_x", "group_core")
GROUP = (FAR,) + NEAR
SECTION = ("section_y", "section_z")


def gather_prefix(block):
    far = lax.axis_size(FAR)
    near = lax.axis_size(NEAR)
    rows, width = block.shape
    spread = jnp.broadcast_to(block[None], (far, rows, width))
    column = lax.all_to_all(spread, FAR, 0, 0, tiled=True).reshape(far * rows, width)
    spread = jnp.broadcast_to(column[None], (near, far * rows, width))
    whole = lax.all_to_all(spread, NEAR, 0, 0, tiled=True)
    whole = whole.reshape(near, far, rows, width).transpose(1, 0, 2, 3)
    return whole.reshape(far * near * rows, width)


def scatter_sum(term, hold):
    far = lax.axis_size(FAR)
    near = lax.axis_size(NEAR)
    slots, width = term.shape
    rows = slots // (far * near)
    parts = term.reshape(far, near, rows, width).transpose(1, 0, 2, 3)
    parts = parts.reshape(near, far * rows, width)
    parts = lax.all_to_all(parts, NEAR, 0, 0, tiled=True).sum(axis=0)
    parts = parts.reshape(far, rows, width)
    parts, hold = lax.optimization_barrier((parts, hold))
    return lax.all_to_all(parts, FAR, 0, 0, tiled=True).sum(axis=0), hold


def from_behind(value, axis, steps):
    count = lax.axis_size(axis)
    pairs = [(source, (source + steps) % count) for source in range(count)]
    return lax.ppermute(value, axis, pairs)


def score_block(q_four, keys):
    total = keys.shape[0]
    k_three = keys.reshape(total, KV_HEADS, HEAD_DIM)
    return jnp.einsum(
        "rgqh,mgh->gqrm", q_four, k_three, preferred_element_type=jnp.float32
    ) * HEAD_DIM ** (-0.5)


def key_terms(d_low, w_low, q_four, d_four, total):
    grad_k = jnp.einsum(
        "gqrm,rgqh->mgh", d_low, q_four, preferred_element_type=jnp.float32
    ) * HEAD_DIM ** (-0.5)
    grad_v = jnp.einsum("gqrm,rgqh->mgh", w_low, d_four, preferred_element_type=jnp.float32)
    return (grad_k.reshape(total, KV_HEADS * HEAD_DIM), grad_v.reshape(total, KV_HEADS * HEAD_DIM))


def per_device(proj_rows, out_grad, prefix_kv, prefix_len, comp_len, owner):
    width = HEADS * HEAD_DIM
    kv_width = KV_HEADS * HEAD_DIM
    per = HEADS // KV_HEADS
    rows = proj_rows[0]
    count = rows.shape[0]
    queries = rows[:, :width]
    own_keys = rows[:, width : width + kv_width]
    own_values = rows[:, width + kv_width :]
    member = (lax.axis_index(FAR) * lax.axis_size(NEAR[0]) + lax.axis_index(NEAR[0])) * lax.axis_size(
        NEAR[1]
    ) + lax.axis_index(NEAR[1])
    groups = lax.axis_size(FAR) * lax.axis_size(NEAR)
    picked = jnp.arange(groups) == member
    prompt = jnp.sum(jnp.where(picked, owner, 0))
    length = jnp.sum(jnp.where(picked, comp_len, 0))
    prompt_count = prefix_len.shape[0]
    prompt_ids = jnp.arange(prompt_count)
    offset = jnp.sum(jnp.where(prompt_ids < prompt, prefix_len, 0))
    span = jnp.sum(jnp.where(prompt_ids == prompt, prefix_len, 0))
    token_ids = jnp.arange(count)
    live = token_ids < length
    dout = jnp.where(live[:, None], out_grad[0], jnp.zeros_like(out_grad[0]))
    gathered = gather_prefix(prefix_kv[0])
    slots = gathered.shape[0]
    window = min(slots, 3 * slots // prompt_count)
    first = jnp.minimum(offset, slots - window)
    window_rows = lax.dynamic_slice_in_dim(gathered, first, window, 0)
    positions = first + jnp.arange(window)
    inside = (positions >= offset) & (positions < offset + span)
    causal = token_ids[:, None] >= token_ids[None, :]
    keys = jnp.concatenate([window_rows[:, :kv_width], own_keys], axis=0)
    values = jnp.concatenate([window_rows[:, kv_width:], own_values], axis=0)
    allowed = jnp.concatenate([jnp.broadcast_to(inside[None, :], (count, window)), causal], axis=1)
    total_keys = window + count
    q_four = queries.reshape(count, KV_HEADS, per, HEAD_DIM)
    d_four = dout.reshape(count, KV_HEADS, per, HEAD_DIM)
    v_three = values.reshape(total_keys, KV_HEADS, HEAD_DIM)
    scores = jnp.where(allowed[None, None], score_block(q_four, keys), jnp.float32(-1e30))
    top = jnp.max(scores, axis=-1, keepdims=True)
    expo = jnp.exp(scores - top)
    denom = jnp.sum(expo, axis=-1, keepdims=True)
    weights = expo / denom
    w_low = weights.astype(jnp.bfloat16)
    output = jnp.einsum("gqrm,mgh->gqrh", w_low, v_three, preferred_element_type=jnp.float32)
    delta = jnp.einsum("rgqh,gqrh->gqr", d_four.astype(jnp.float32), output)
    dprob = jnp.einsum("rgqh,mgh->gqrm", d_four, v_three, preferred_element_type=jnp.float32)
    d_low = (weights * (dprob - delta[..., None])).astype(jnp.bfloat16)
    k_three = keys.reshape(total_keys, KV_HEADS, HEAD_DIM)
    grad_q = jnp.einsum(
        "gqrm,mgh->rgqh", d_low, k_three, preferred_element_type=jnp.float32
    ) * HEAD_DIM ** (-0.5)
    grad_q = grad_q.reshape(count, width).astype(jnp.bfloat16)
    grad_own_k, grad_own_v = key_terms(
        d_low[..., window:], w_low[..., window:], q_four, d_four, count
    )
    own_grad = jnp.concatenate([grad_own_k, grad_own_v], axis=1).astype(jnp.bfloat16)
    passed = from_behind(grad_q[None], SECTION, -1)
    grad_pk, grad_pv = key_terms(d_low[..., :window], w_low[..., :window], q_four, d_four, window)
    window_term = jnp.concatenate([grad_pk, grad_pv], axis=1)
    full_term = lax.dynamic_update_slice_in_dim(
        jnp.zeros((slots, 2 * kv_width), jnp.float32), window_term, first, 0
    )
    prefix_grad, passed = scatter_sum(full_term, passed)
    return (passed, own_grad[None], prefix_grad.astype(jnp.bfloat16)[None])


def solution(mesh):
    group_size = mesh.shape["group"]
    section_size = mesh.shape["section"]
    near_x, near_core = 4, 2
    layout = mesh.devices.reshape(
        group_size // (near_x * near_core), near_x, near_core, section_size // 4, 4
    )
    split = Mesh(layout, GROUP + SECTION)
    placed = P(SECTION, GROUP, None)
    in_specs = (placed, placed, placed, P(), P(), P())
    out_specs = (placed, placed, placed)
    return jax.shard_map(
        per_device, mesh=split, in_specs=in_specs, out_specs=out_specs, check_vma=False
    )
```

```python
import jax
import jax.numpy as jnp
from jax import lax
from jax.sharding import Mesh, PartitionSpec as P

HEADS = 16
KV_HEADS = 2
HEAD_DIM = 128

FAR = "group_z"
NEAR = ("group_x", "group_core")
GROUP = (FAR,) + NEAR
SECTION = ("section_y", "section_z")


def gather_prefix(block):
    far = lax.axis_size(FAR)
    near = lax.axis_size(NEAR)
    rows, width = block.shape
    spread = jnp.broadcast_to(block[None], (far, rows, width))
    column = lax.all_to_all(spread, FAR, 0, 0, tiled=True).reshape(far * rows, width)
    spread = jnp.broadcast_to(column[None], (near, far * rows, width))
    whole = lax.all_to_all(spread, NEAR, 0, 0, tiled=True)
    whole = whole.reshape(near, far, rows, width).transpose(1, 0, 2, 3)
    return whole.reshape(far * near * rows, width)


def scatter_sum(term):
    far = lax.axis_size(FAR)
    near = lax.axis_size(NEAR)
    slots, width = term.shape
    rows = slots // (far * near)
    parts = term.reshape(far, near, rows, width).transpose(1, 0, 2, 3)
    parts = parts.reshape(near, far * rows, width)
    parts = lax.all_to_all(parts, NEAR, 0, 0, tiled=True).sum(axis=0)
    parts = parts.reshape(far, rows, width)
    return lax.all_to_all(parts, FAR, 0, 0, tiled=True).sum(axis=0)


def from_behind(value, axis, steps):
    count = lax.axis_size(axis)
    pairs = [(source, (source + steps) % count) for source in range(count)]
    return lax.ppermute(value, axis, pairs)


def score_block(q_four, keys):
    total = keys.shape[0]
    k_three = keys.reshape(total, KV_HEADS, HEAD_DIM)
    return jnp.einsum(
        "rgqh,mgh->gqrm", q_four, k_three, preferred_element_type=jnp.float32
    ) * HEAD_DIM ** (-0.5)


def key_terms(d_low, w_low, q_four, d_four, total):
    grad_k = jnp.einsum(
        "gqrm,rgqh->mgh", d_low, q_four, preferred_element_type=jnp.float32
    ) * HEAD_DIM ** (-0.5)
    grad_v = jnp.einsum("gqrm,rgqh->mgh", w_low, d_four, preferred_element_type=jnp.float32)
    return (grad_k.reshape(total, KV_HEADS * HEAD_DIM), grad_v.reshape(total, KV_HEADS * HEAD_DIM))


def per_device(proj_rows, out_grad, prefix_kv, prefix_len, comp_len, owner):
    width = HEADS * HEAD_DIM
    kv_width = KV_HEADS * HEAD_DIM
    per = HEADS // KV_HEADS
    rows = proj_rows[0]
    count = rows.shape[0]
    queries = rows[:, :width]
    own_keys = rows[:, width : width + kv_width]
    own_values = rows[:, width + kv_width :]
    member = (lax.axis_index(FAR) * lax.axis_size(NEAR[0]) + lax.axis_index(NEAR[0])) * lax.axis_size(
        NEAR[1]
    ) + lax.axis_index(NEAR[1])
    groups = lax.axis_size(FAR) * lax.axis_size(NEAR)
    picked = jnp.arange(groups) == member
    prompt = jnp.sum(jnp.where(picked, owner, 0))
    length = jnp.sum(jnp.where(picked, comp_len, 0))
    prompt_count = prefix_len.shape[0]
    prompt_ids = jnp.arange(prompt_count)
    offset = jnp.sum(jnp.where(prompt_ids < prompt, prefix_len, 0))
    span = jnp.sum(jnp.where(prompt_ids == prompt, prefix_len, 0))
    token_ids = jnp.arange(count)
    live = token_ids < length
    dout = jnp.where(live[:, None], out_grad[0], jnp.zeros_like(out_grad[0]))
    gathered = gather_prefix(prefix_kv[0])
    slots = gathered.shape[0]
    window = min(slots, 3 * slots // prompt_count)
    first = jnp.minimum(offset, slots - window)
    window_rows = lax.dynamic_slice_in_dim(gathered, first, window, 0)
    positions = first + jnp.arange(window)
    inside = (positions >= offset) & (positions < offset + span)
    causal = token_ids[:, None] >= token_ids[None, :]
    keys = jnp.concatenate([window_rows[:, :kv_width], own_keys], axis=0)
    values = jnp.concatenate([window_rows[:, kv_width:], own_values], axis=0)
    allowed = jnp.concatenate([jnp.broadcast_to(inside[None, :], (count, window)), causal], axis=1)
    total_keys = window + count
    q_four = queries.reshape(count, KV_HEADS, per, HEAD_DIM)
    d_four = dout.reshape(count, KV_HEADS, per, HEAD_DIM)
    v_three = values.reshape(total_keys, KV_HEADS, HEAD_DIM)
    scores = jnp.where(allowed[None, None], score_block(q_four, keys), jnp.float32(-1e30))
    top = jnp.max(scores, axis=-1, keepdims=True)
    expo = jnp.exp(scores - top)
    denom = jnp.sum(expo, axis=-1, keepdims=True)
    weights = expo / denom
    w_low = weights.astype(jnp.bfloat16)
    output = jnp.einsum("gqrm,mgh->gqrh", w_low, v_three, preferred_element_type=jnp.float32)
    delta = jnp.einsum("rgqh,gqrh->gqr", d_four.astype(jnp.float32), output)
    dprob = jnp.einsum("rgqh,mgh->gqrm", d_four, v_three, preferred_element_type=jnp.float32)
    d_low = (weights * (dprob - delta[..., None])).astype(jnp.bfloat16)
    k_three = keys.reshape(total_keys, KV_HEADS, HEAD_DIM)
    grad_q = jnp.einsum(
        "gqrm,mgh->rgqh", d_low, k_three, preferred_element_type=jnp.float32
    ) * HEAD_DIM ** (-0.5)
    grad_q = grad_q.reshape(count, width).astype(jnp.bfloat16)
    passed = from_behind(grad_q[None], SECTION, -1)
    grad_pk, grad_pv = key_terms(d_low[..., :window], w_low[..., :window], q_four, d_four, window)
    window_term = jnp.concatenate([grad_pk, grad_pv], axis=1)
    full_term = lax.dynamic_update_slice_in_dim(
        jnp.zeros((slots, 2 * kv_width), jnp.float32), window_term, first, 0
    )
    prefix_grad = scatter_sum(full_term)
    passed, d_own, w_own = lax.optimization_barrier((passed, d_low[..., window:], w_low[..., window:]))
    grad_own_k, grad_own_v = key_terms(d_own, w_own, q_four, d_four, count)
    own_grad = jnp.concatenate([grad_own_k, grad_own_v], axis=1).astype(jnp.bfloat16)
    return (passed, own_grad[None], prefix_grad.astype(jnp.bfloat16)[None])


def solution(mesh):
    group_size = mesh.shape["group"]
    section_size = mesh.shape["section"]
    near_x, near_core = 4, 2
    layout = mesh.devices.reshape(
        group_size // (near_x * near_core), near_x, near_core, section_size // 4, 4
    )
    split = Mesh(layout, GROUP + SECTION)
    placed = P(SECTION, GROUP, None)
    in_specs = (placed, placed, placed, P(), P(), P())
    out_specs = (placed, placed, placed)
    return jax.shard_map(
        per_device, mesh=split, in_specs=in_specs, out_specs=out_specs, check_vma=False
    )
```

```python
import jax
import jax.numpy as jnp
from jax import lax
from jax.sharding import Mesh, PartitionSpec as P

HEADS = 16
KV_HEADS = 2
HEAD_DIM = 128

FAR = "group_z"
NEAR = ("group_x", "group_core")
GROUP = (FAR,) + NEAR
SECTION = ("section_y", "section_z")


def gather_prefix(block):
    far = lax.axis_size(FAR)
    near = lax.axis_size(NEAR)
    rows, width = block.shape
    spread = jnp.broadcast_to(block[None], (far, rows, width))
    column = lax.all_to_all(spread, FAR, 0, 0, tiled=True).reshape(far * rows, width)
    spread = jnp.broadcast_to(column[None], (near, far * rows, width))
    whole = lax.all_to_all(spread, NEAR, 0, 0, tiled=True)
    whole = whole.reshape(near, far, rows, width).transpose(1, 0, 2, 3)
    return whole.reshape(far * near * rows, width)


def scatter_sum(term):
    far = lax.axis_size(FAR)
    near = lax.axis_size(NEAR)
    slots, width = term.shape
    rows = slots // (far * near)
    parts = term.reshape(far, near, rows, width).transpose(1, 0, 2, 3)
    parts = parts.reshape(near, far * rows, width)
    parts = lax.all_to_all(parts, NEAR, 0, 0, tiled=True).sum(axis=0)
    parts = parts.reshape(far, rows, width)
    return lax.all_to_all(parts, FAR, 0, 0, tiled=True).sum(axis=0)


def around(count, far_count, move):
    pairs = []
    for source in range(count):
        near, far = divmod(source, far_count)
        near, far = move(near, far)
        pairs.append((source, (near % (count // far_count)) * far_count + far % far_count))
    return pairs


def pass_down(value, axis):
    count = lax.axis_size(axis)
    far_count = lax.axis_size(axis[1])
    rows = value.shape[1]
    cut = rows - rows // 8
    direct = lax.ppermute(value[:, :cut], axis, around(count, far_count, lambda n, f: (n - (f == 0), f - 1)))
    rest = value[:, cut:]
    hop = around(count, far_count, lambda n, f: (n, f + 1))
    rest = lax.ppermute(rest, axis, hop)
    rest = lax.ppermute(rest, axis, hop)
    last = around(count, far_count, lambda n, f: (n - (f == 2), f + 1))
    rest = lax.ppermute(rest, axis, last)
    return jnp.concatenate([direct, rest], axis=1)


def from_behind(value, axis, steps):
    count = lax.axis_size(axis)
    pairs = [(source, (source + steps) % count) for source in range(count)]
    return lax.ppermute(value, axis, pairs)


def score_block(q_four, keys):
    total = keys.shape[0]
    k_three = keys.reshape(total, KV_HEADS, HEAD_DIM)
    return jnp.einsum(
        "rgqh,mgh->gqrm", q_four, k_three, preferred_element_type=jnp.float32
    ) * HEAD_DIM ** (-0.5)


def key_terms(d_low, w_low, q_four, d_four, total):
    grad_k = jnp.einsum(
        "gqrm,rgqh->mgh", d_low, q_four, preferred_element_type=jnp.float32
    ) * HEAD_DIM ** (-0.5)
    grad_v = jnp.einsum("gqrm,rgqh->mgh", w_low, d_four, preferred_element_type=jnp.float32)
    return (grad_k.reshape(total, KV_HEADS * HEAD_DIM), grad_v.reshape(total, KV_HEADS * HEAD_DIM))


def per_device(proj_rows, out_grad, prefix_kv, prefix_len, comp_len, owner):
    width = HEADS * HEAD_DIM
    kv_width = KV_HEADS * HEAD_DIM
    per = HEADS // KV_HEADS
    rows = proj_rows[0]
    count = rows.shape[0]
    queries = rows[:, :width]
    own_keys = rows[:, width : width + kv_width]
    own_values = rows[:, width + kv_width :]
    member = (lax.axis_index(FAR) * lax.axis_size(NEAR[0]) + lax.axis_index(NEAR[0])) * lax.axis_size(
        NEAR[1]
    ) + lax.axis_index(NEAR[1])
    groups = lax.axis_size(FAR) * lax.axis_size(NEAR)
    picked = jnp.arange(groups) == member
    prompt = jnp.sum(jnp.where(picked, owner, 0))
    length = jnp.sum(jnp.where(picked, comp_len, 0))
    prompt_count = prefix_len.shape[0]
    prompt_ids = jnp.arange(prompt_count)
    offset = jnp.sum(jnp.where(prompt_ids < prompt, prefix_len, 0))
    span = jnp.sum(jnp.where(prompt_ids == prompt, prefix_len, 0))
    token_ids = jnp.arange(count)
    live = token_ids < length
    dout = jnp.where(live[:, None], out_grad[0], jnp.zeros_like(out_grad[0]))
    gathered = gather_prefix(prefix_kv[0])
    slots = gathered.shape[0]
    window = min(slots, 3 * slots // prompt_count)
    first = jnp.minimum(offset, slots - window)
    window_rows = lax.dynamic_slice_in_dim(gathered, first, window, 0)
    positions = first + jnp.arange(window)
    inside = (positions >= offset) & (positions < offset + span)
    causal = token_ids[:, None] >= token_ids[None, :]
    keys = jnp.concatenate([window_rows[:, :kv_width], own_keys], axis=0)
    values = jnp.concatenate([window_rows[:, kv_width:], own_values], axis=0)
    allowed = jnp.concatenate([jnp.broadcast_to(inside[None, :], (count, window)), causal], axis=1)
    total_keys = window + count
    q_four = queries.reshape(count, KV_HEADS, per, HEAD_DIM)
    d_four = dout.reshape(count, KV_HEADS, per, HEAD_DIM)
    v_three = values.reshape(total_keys, KV_HEADS, HEAD_DIM)
    scores = jnp.where(allowed[None, None], score_block(q_four, keys), jnp.float32(-1e30))
    top = jnp.max(scores, axis=-1, keepdims=True)
    expo = jnp.exp(scores - top)
    denom = jnp.sum(expo, axis=-1, keepdims=True)
    weights = expo / denom
    w_low = weights.astype(jnp.bfloat16)
    output = jnp.einsum("gqrm,mgh->gqrh", w_low, v_three, preferred_element_type=jnp.float32)
    delta = jnp.einsum("rgqh,gqrh->gqr", d_four.astype(jnp.float32), output)
    dprob = jnp.einsum("rgqh,mgh->gqrm", d_four, v_three, preferred_element_type=jnp.float32)
    d_low = (weights * (dprob - delta[..., None])).astype(jnp.bfloat16)
    k_three = keys.reshape(total_keys, KV_HEADS, HEAD_DIM)
    grad_q = jnp.einsum(
        "gqrm,mgh->rgqh", d_low, k_three, preferred_element_type=jnp.float32
    ) * HEAD_DIM ** (-0.5)
    grad_q = grad_q.reshape(count, width).astype(jnp.bfloat16)
    passed = pass_down(grad_q[None], SECTION)
    grad_pk, grad_pv = key_terms(d_low[..., :window], w_low[..., :window], q_four, d_four, window)
    window_term = jnp.concatenate([grad_pk, grad_pv], axis=1)
    full_term = lax.dynamic_update_slice_in_dim(
        jnp.zeros((slots, 2 * kv_width), jnp.float32), window_term, first, 0
    )
    prefix_grad = scatter_sum(full_term)
    passed, d_own, w_own = lax.optimization_barrier((passed, d_low[..., window:], w_low[..., window:]))
    grad_own_k, grad_own_v = key_terms(d_own, w_own, q_four, d_four, count)
    own_grad = jnp.concatenate([grad_own_k, grad_own_v], axis=1).astype(jnp.bfloat16)
    return (passed, own_grad[None], prefix_grad.astype(jnp.bfloat16)[None])


def solution(mesh):
    group_size = mesh.shape["group"]
    section_size = mesh.shape["section"]
    near_x, near_core = 4, 2
    layout = mesh.devices.reshape(
        group_size // (near_x * near_core), near_x, near_core, section_size // 4, 4
    )
    split = Mesh(layout, GROUP + SECTION)
    placed = P(SECTION, GROUP, None)
    in_specs = (placed, placed, placed, P(), P(), P())
    out_specs = (placed, placed, placed)
    return jax.shard_map(
        per_device, mesh=split, in_specs=in_specs, out_specs=out_specs, check_vma=False
    )
```

```python
import jax
import jax.numpy as jnp
from jax import lax
from jax.sharding import Mesh, PartitionSpec as P

HEADS = 16
KV_HEADS = 2
HEAD_DIM = 128

FAR = "group_z"
NEAR = ("group_x", "group_core")
GROUP = (FAR,) + NEAR
SECTION = ("section_y", "section_z")


def gather_prefix(block):
    far = lax.axis_size(FAR)
    near = lax.axis_size(NEAR)
    rows, width = block.shape
    spread = jnp.broadcast_to(block[None], (far, rows, width))
    column = lax.all_to_all(spread, FAR, 0, 0, tiled=True).reshape(far * rows, width)
    spread = jnp.broadcast_to(column[None], (near, far * rows, width))
    whole = lax.all_to_all(spread, NEAR, 0, 0, tiled=True)
    whole = whole.reshape(near, far, rows, width).transpose(1, 0, 2, 3)
    return whole.reshape(far * near * rows, width)


def scatter_sum(term):
    far = lax.axis_size(FAR)
    near = lax.axis_size(NEAR)
    slots, width = term.shape
    rows = slots // (far * near)
    parts = term.reshape(far, near, rows, width).transpose(1, 0, 2, 3)
    parts = parts.reshape(near, far * rows, width)
    parts = lax.all_to_all(parts, NEAR, 0, 0, tiled=True).sum(axis=0)
    parts = parts.reshape(far, rows, width)
    return lax.all_to_all(parts, FAR, 0, 0, tiled=True).sum(axis=0)


def around(count, far_count, move):
    pairs = []
    for source in range(count):
        near, far = divmod(source, far_count)
        near, far = move(near, far)
        pairs.append((source, (near % (count // far_count)) * far_count + far % far_count))
    return pairs


def pass_down(value, axis):
    count = lax.axis_size(axis)
    far_count = lax.axis_size(axis[1])
    rows = value.shape[1]
    cut = rows - 3 * rows // 16
    direct = lax.ppermute(value[:, :cut], axis, around(count, far_count, lambda n, f: (n - (f == 0), f - 1)))
    rest = value[:, cut:]
    hop = around(count, far_count, lambda n, f: (n, f + 1))
    rest = lax.ppermute(rest, axis, hop)
    rest = lax.ppermute(rest, axis, hop)
    last = around(count, far_count, lambda n, f: (n - (f == 2), f + 1))
    rest = lax.ppermute(rest, axis, last)
    return jnp.concatenate([direct, rest], axis=1)


def from_behind(value, axis, steps):
    count = lax.axis_size(axis)
    pairs = [(source, (source + steps) % count) for source in range(count)]
    return lax.ppermute(value, axis, pairs)


def score_block(q_four, keys):
    total = keys.shape[0]
    k_three = keys.reshape(total, KV_HEADS, HEAD_DIM)
    return jnp.einsum(
        "rgqh,mgh->gqrm", q_four, k_three, preferred_element_type=jnp.float32
    ) * HEAD_DIM ** (-0.5)


def key_terms(d_low, w_low, q_four, d_four, total):
    grad_k = jnp.einsum(
        "gqrm,rgqh->mgh", d_low, q_four, preferred_element_type=jnp.float32
    ) * HEAD_DIM ** (-0.5)
    grad_v = jnp.einsum("gqrm,rgqh->mgh", w_low, d_four, preferred_element_type=jnp.float32)
    return (grad_k.reshape(total, KV_HEADS * HEAD_DIM), grad_v.reshape(total, KV_HEADS * HEAD_DIM))


def per_device(proj_rows, out_grad, prefix_kv, prefix_len, comp_len, owner):
    width = HEADS * HEAD_DIM
    kv_width = KV_HEADS * HEAD_DIM
    per = HEADS // KV_HEADS
    rows = proj_rows[0]
    count = rows.shape[0]
    queries = rows[:, :width]
    own_keys = rows[:, width : width + kv_width]
    own_values = rows[:, width + kv_width :]
    member = (lax.axis_index(FAR) * lax.axis_size(NEAR[0]) + lax.axis_index(NEAR[0])) * lax.axis_size(
        NEAR[1]
    ) + lax.axis_index(NEAR[1])
    groups = lax.axis_size(FAR) * lax.axis_size(NEAR)
    picked = jnp.arange(groups) == member
    prompt = jnp.sum(jnp.where(picked, owner, 0))
    length = jnp.sum(jnp.where(picked, comp_len, 0))
    prompt_count = prefix_len.shape[0]
    prompt_ids = jnp.arange(prompt_count)
    offset = jnp.sum(jnp.where(prompt_ids < prompt, prefix_len, 0))
    span = jnp.sum(jnp.where(prompt_ids == prompt, prefix_len, 0))
    token_ids = jnp.arange(count)
    live = token_ids < length
    dout = jnp.where(live[:, None], out_grad[0], jnp.zeros_like(out_grad[0]))
    gathered = gather_prefix(prefix_kv[0])
    slots = gathered.shape[0]
    window = min(slots, 3 * slots // prompt_count)
    first = jnp.minimum(offset, slots - window)
    window_rows = lax.dynamic_slice_in_dim(gathered, first, window, 0)
    positions = first + jnp.arange(window)
    inside = (positions >= offset) & (positions < offset + span)
    causal = token_ids[:, None] >= token_ids[None, :]
    keys = jnp.concatenate([window_rows[:, :kv_width], own_keys], axis=0)
    values = jnp.concatenate([window_rows[:, kv_width:], own_values], axis=0)
    allowed = jnp.concatenate([jnp.broadcast_to(inside[None, :], (count, window)), causal], axis=1)
    total_keys = window + count
    q_four = queries.reshape(count, KV_HEADS, per, HEAD_DIM)
    d_four = dout.reshape(count, KV_HEADS, per, HEAD_DIM)
    v_three = values.reshape(total_keys, KV_HEADS, HEAD_DIM)
    scores = jnp.where(allowed[None, None], score_block(q_four, keys), jnp.float32(-1e30))
    top = jnp.max(scores, axis=-1, keepdims=True)
    expo = jnp.exp(scores - top)
    denom = jnp.sum(expo, axis=-1, keepdims=True)
    weights = expo / denom
    w_low = weights.astype(jnp.bfloat16)
    output = jnp.einsum("gqrm,mgh->gqrh", w_low, v_three, preferred_element_type=jnp.float32)
    delta = jnp.einsum("rgqh,gqrh->gqr", d_four.astype(jnp.float32), output)
    dprob = jnp.einsum("rgqh,mgh->gqrm", d_four, v_three, preferred_element_type=jnp.float32)
    d_low = (weights * (dprob - delta[..., None])).astype(jnp.bfloat16)
    k_three = keys.reshape(total_keys, KV_HEADS, HEAD_DIM)
    grad_q = jnp.einsum(
        "gqrm,mgh->rgqh", d_low, k_three, preferred_element_type=jnp.float32
    ) * HEAD_DIM ** (-0.5)
    grad_q = grad_q.reshape(count, width).astype(jnp.bfloat16)
    passed = pass_down(grad_q[None], SECTION)
    grad_pk, grad_pv = key_terms(d_low[..., :window], w_low[..., :window], q_four, d_four, window)
    window_term = jnp.concatenate([grad_pk, grad_pv], axis=1)
    full_term = lax.dynamic_update_slice_in_dim(
        jnp.zeros((slots, 2 * kv_width), jnp.float32), window_term, first, 0
    )
    prefix_grad = scatter_sum(full_term)
    passed, d_own, w_own = lax.optimization_barrier((passed, d_low[..., window:], w_low[..., window:]))
    grad_own_k, grad_own_v = key_terms(d_own, w_own, q_four, d_four, count)
    own_grad = jnp.concatenate([grad_own_k, grad_own_v], axis=1).astype(jnp.bfloat16)
    return (passed, own_grad[None], prefix_grad.astype(jnp.bfloat16)[None])


def solution(mesh):
    group_size = mesh.shape["group"]
    section_size = mesh.shape["section"]
    near_x, near_core = 4, 2
    layout = mesh.devices.reshape(
        group_size // (near_x * near_core), near_x, near_core, section_size // 4, 4
    )
    split = Mesh(layout, GROUP + SECTION)
    placed = P(SECTION, GROUP, None)
    in_specs = (placed, placed, placed, P(), P(), P())
    out_specs = (placed, placed, placed)
    return jax.shard_map(
        per_device, mesh=split, in_specs=in_specs, out_specs=out_specs, check_vma=False
    )
```

```python
import jax
import jax.numpy as jnp
from jax import lax
from jax.sharding import Mesh, PartitionSpec as P

HEADS = 16
KV_HEADS = 2
HEAD_DIM = 128

FAR = "group_z"
NEAR = ("group_x", "group_core")
GROUP = (FAR,) + NEAR
SECTION = ("section_y", "section_z")


def gather_prefix(block, hold):
    far = lax.axis_size(FAR)
    near = lax.axis_size(NEAR)
    rows, width = block.shape
    spread = jnp.broadcast_to(block[None], (far, rows, width))
    column = lax.all_to_all(spread, FAR, 0, 0, tiled=True).reshape(far * rows, width)
    column, hold = lax.optimization_barrier((column, hold))
    spread = jnp.broadcast_to(column[None], (near, far * rows, width))
    whole = lax.all_to_all(spread, NEAR, 0, 0, tiled=True)
    whole = whole.reshape(near, far, rows, width).transpose(1, 0, 2, 3)
    return whole.reshape(far * near * rows, width), hold


def scatter_sum(term):
    far = lax.axis_size(FAR)
    near = lax.axis_size(NEAR)
    slots, width = term.shape
    rows = slots // (far * near)
    parts = term.reshape(far, near, rows, width).transpose(1, 0, 2, 3)
    parts = parts.reshape(near, far * rows, width)
    parts = lax.all_to_all(parts, NEAR, 0, 0, tiled=True).sum(axis=0)
    parts = parts.reshape(far, rows, width)
    return lax.all_to_all(parts, FAR, 0, 0, tiled=True).sum(axis=0)


def around(count, far_count, move):
    pairs = []
    for source in range(count):
        near, far = divmod(source, far_count)
        near, far = move(near, far)
        pairs.append((source, (near % (count // far_count)) * far_count + far % far_count))
    return pairs


def pass_down(value, axis):
    count = lax.axis_size(axis)
    far_count = lax.axis_size(axis[1])
    rows = value.shape[1]
    cut = rows - 3 * rows // 16
    direct = lax.ppermute(value[:, :cut], axis, around(count, far_count, lambda n, f: (n - (f == 0), f - 1)))
    rest = value[:, cut:]
    hop = around(count, far_count, lambda n, f: (n, f + 1))
    rest = lax.ppermute(rest, axis, hop)
    rest = lax.ppermute(rest, axis, hop)
    last = around(count, far_count, lambda n, f: (n - (f == 2), f + 1))
    rest = lax.ppermute(rest, axis, last)
    return jnp.concatenate([direct, rest], axis=1)


def from_behind(value, axis, steps):
    count = lax.axis_size(axis)
    pairs = [(source, (source + steps) % count) for source in range(count)]
    return lax.ppermute(value, axis, pairs)


def score_block(q_four, keys):
    total = keys.shape[0]
    k_three = keys.reshape(total, KV_HEADS, HEAD_DIM)
    return jnp.einsum(
        "rgqh,mgh->gqrm", q_four, k_three, preferred_element_type=jnp.float32
    ) * HEAD_DIM ** (-0.5)


def key_terms(d_low, w_low, q_four, d_four, total):
    grad_k = jnp.einsum(
        "gqrm,rgqh->mgh", d_low, q_four, preferred_element_type=jnp.float32
    ) * HEAD_DIM ** (-0.5)
    grad_v = jnp.einsum("gqrm,rgqh->mgh", w_low, d_four, preferred_element_type=jnp.float32)
    return (grad_k.reshape(total, KV_HEADS * HEAD_DIM), grad_v.reshape(total, KV_HEADS * HEAD_DIM))


def per_device(proj_rows, out_grad, prefix_kv, prefix_len, comp_len, owner):
    width = HEADS * HEAD_DIM
    kv_width = KV_HEADS * HEAD_DIM
    per = HEADS // KV_HEADS
    rows = proj_rows[0]
    count = rows.shape[0]
    queries = rows[:, :width]
    own_keys = rows[:, width : width + kv_width]
    own_values = rows[:, width + kv_width :]
    member = (lax.axis_index(FAR) * lax.axis_size(NEAR[0]) + lax.axis_index(NEAR[0])) * lax.axis_size(
        NEAR[1]
    ) + lax.axis_index(NEAR[1])
    groups = lax.axis_size(FAR) * lax.axis_size(NEAR)
    picked = jnp.arange(groups) == member
    prompt = jnp.sum(jnp.where(picked, owner, 0))
    length = jnp.sum(jnp.where(picked, comp_len, 0))
    prompt_count = prefix_len.shape[0]
    prompt_ids = jnp.arange(prompt_count)
    offset = jnp.sum(jnp.where(prompt_ids < prompt, prefix_len, 0))
    span = jnp.sum(jnp.where(prompt_ids == prompt, prefix_len, 0))
    token_ids = jnp.arange(count)
    live = token_ids < length
    dout = jnp.where(live[:, None], out_grad[0], jnp.zeros_like(out_grad[0]))
    met = lax.ppermute(prefix_kv[0][:8, :128], SECTION, around(
        lax.axis_size(SECTION), lax.axis_size(SECTION[1]), lambda n, f: (n - (f == 0), f - 1)))
    gathered, met = gather_prefix(prefix_kv[0], met)
    slots = gathered.shape[0]
    window = min(slots, 3 * slots // prompt_count)
    first = jnp.minimum(offset, slots - window)
    window_rows = lax.dynamic_slice_in_dim(gathered, first, window, 0)
    positions = first + jnp.arange(window)
    inside = (positions >= offset) & (positions < offset + span)
    causal = token_ids[:, None] >= token_ids[None, :]
    keys = jnp.concatenate([window_rows[:, :kv_width], own_keys], axis=0)
    values = jnp.concatenate([window_rows[:, kv_width:], own_values], axis=0)
    allowed = jnp.concatenate([jnp.broadcast_to(inside[None, :], (count, window)), causal], axis=1)
    total_keys = window + count
    q_four = queries.reshape(count, KV_HEADS, per, HEAD_DIM)
    d_four = dout.reshape(count, KV_HEADS, per, HEAD_DIM)
    v_three = values.reshape(total_keys, KV_HEADS, HEAD_DIM)
    scores = jnp.where(allowed[None, None], score_block(q_four, keys), jnp.float32(-1e30))
    top = jnp.max(scores, axis=-1, keepdims=True)
    expo = jnp.exp(scores - top)
    denom = jnp.sum(expo, axis=-1, keepdims=True)
    weights = expo / denom
    w_low = weights.astype(jnp.bfloat16)
    output = jnp.einsum("gqrm,mgh->gqrh", w_low, v_three, preferred_element_type=jnp.float32)
    delta = jnp.einsum("rgqh,gqrh->gqr", d_four.astype(jnp.float32), output)
    dprob = jnp.einsum("rgqh,mgh->gqrm", d_four, v_three, preferred_element_type=jnp.float32)
    d_low = (weights * (dprob - delta[..., None])).astype(jnp.bfloat16)
    k_three = keys.reshape(total_keys, KV_HEADS, HEAD_DIM)
    grad_q = jnp.einsum(
        "gqrm,mgh->rgqh", d_low, k_three, preferred_element_type=jnp.float32
    ) * HEAD_DIM ** (-0.5)
    grad_q = grad_q.reshape(count, width).astype(jnp.bfloat16)
    passed = pass_down(grad_q[None], SECTION)
    grad_pk, grad_pv = key_terms(d_low[..., :window], w_low[..., :window], q_four, d_four, window)
    window_term = jnp.concatenate([grad_pk, grad_pv], axis=1)
    full_term = lax.dynamic_update_slice_in_dim(
        jnp.zeros((slots, 2 * kv_width), jnp.float32), window_term, first, 0
    )
    prefix_grad = scatter_sum(full_term)
    passed, d_own, w_own, met = lax.optimization_barrier(
        (passed, d_low[..., window:], w_low[..., window:], met)
    )
    grad_own_k, grad_own_v = key_terms(d_own, w_own, q_four, d_four, count)
    own_grad = jnp.concatenate([grad_own_k, grad_own_v], axis=1).astype(jnp.bfloat16)
    prefix_grad = jnp.where(met[0, 0] == jnp.inf, jnp.zeros_like(prefix_grad), prefix_grad)
    return (passed, own_grad[None], prefix_grad.astype(jnp.bfloat16)[None])


def solution(mesh):
    group_size = mesh.shape["group"]
    section_size = mesh.shape["section"]
    near_x, near_core = 4, 2
    layout = mesh.devices.reshape(
        group_size // (near_x * near_core), near_x, near_core, section_size // 4, 4
    )
    split = Mesh(layout, GROUP + SECTION)
    placed = P(SECTION, GROUP, None)
    in_specs = (placed, placed, placed, P(), P(), P())
    out_specs = (placed, placed, placed)
    return jax.shard_map(
        per_device, mesh=split, in_specs=in_specs, out_specs=out_specs, check_vma=False
    )
```

```python
import jax
import jax.numpy as jnp
from jax import lax
from jax.sharding import Mesh, PartitionSpec as P

HEADS = 16
KV_HEADS = 2
HEAD_DIM = 128

FAR = "group_z"
NEAR = ("group_x", "group_core")
GROUP = (FAR,) + NEAR
SECTION = ("section_y", "section_z")


def gather_prefix(block):
    far = lax.axis_size(FAR)
    near = lax.axis_size(NEAR)
    rows, width = block.shape
    spread = jnp.broadcast_to(block[None], (far, rows, width))
    column = lax.all_to_all(spread, FAR, 0, 0, tiled=True).reshape(far * rows, width)
    spread = jnp.broadcast_to(column[None], (near, far * rows, width))
    whole = lax.all_to_all(spread, NEAR, 0, 0, tiled=True)
    whole = whole.reshape(near, far, rows, width).transpose(1, 0, 2, 3)
    return whole.reshape(far * near * rows, width)


def scatter_near(term):
    far = lax.axis_size(FAR)
    near = lax.axis_size(NEAR)
    slots, width = term.shape
    rows = slots // (far * near)
    parts = term.reshape(far, near, rows, width).transpose(1, 0, 2, 3)
    parts = parts.reshape(near, far * rows, width)
    parts = lax.all_to_all(parts, NEAR, 0, 0, tiled=True).sum(axis=0)
    return parts.reshape(far, rows, width)


def scatter_far(parts):
    return lax.all_to_all(parts, FAR, 0, 0, tiled=True).sum(axis=0)


def around(count, far_count, move):
    pairs = []
    for source in range(count):
        near, far = divmod(source, far_count)
        near, far = move(near, far)
        pairs.append((source, (near % (count // far_count)) * far_count + far % far_count))
    return pairs


def pass_down(value, axis):
    count = lax.axis_size(axis)
    far_count = lax.axis_size(axis[1])
    rows = value.shape[1]
    cut = rows - 3 * rows // 16
    direct = lax.ppermute(value[:, :cut], axis, around(count, far_count, lambda n, f: (n - (f == 0), f - 1)))
    rest = value[:, cut:]
    hop = around(count, far_count, lambda n, f: (n, f + 1))
    rest = lax.ppermute(rest, axis, hop)
    rest = lax.ppermute(rest, axis, hop)
    last = around(count, far_count, lambda n, f: (n - (f == 2), f + 1))
    rest = lax.ppermute(rest, axis, last)
    return jnp.concatenate([direct, rest], axis=1)


def from_behind(value, axis, steps):
    count = lax.axis_size(axis)
    pairs = [(source, (source + steps) % count) for source in range(count)]
    return lax.ppermute(value, axis, pairs)


def score_block(q_four, keys):
    total = keys.shape[0]
    k_three = keys.reshape(total, KV_HEADS, HEAD_DIM)
    return jnp.einsum(
        "rgqh,mgh->gqrm", q_four, k_three, preferred_element_type=jnp.float32
    ) * HEAD_DIM ** (-0.5)


def key_terms(d_low, w_low, q_four, d_four, total):
    grad_k = jnp.einsum(
        "gqrm,rgqh->mgh", d_low, q_four, preferred_element_type=jnp.float32
    ) * HEAD_DIM ** (-0.5)
    grad_v = jnp.einsum("gqrm,rgqh->mgh", w_low, d_four, preferred_element_type=jnp.float32)
    return (grad_k.reshape(total, KV_HEADS * HEAD_DIM), grad_v.reshape(total, KV_HEADS * HEAD_DIM))


def per_device(proj_rows, out_grad, prefix_kv, prefix_len, comp_len, owner):
    width = HEADS * HEAD_DIM
    kv_width = KV_HEADS * HEAD_DIM
    per = HEADS // KV_HEADS
    rows = proj_rows[0]
    count = rows.shape[0]
    queries = rows[:, :width]
    own_keys = rows[:, width : width + kv_width]
    own_values = rows[:, width + kv_width :]
    member = (lax.axis_index(FAR) * lax.axis_size(NEAR[0]) + lax.axis_index(NEAR[0])) * lax.axis_size(
        NEAR[1]
    ) + lax.axis_index(NEAR[1])
    groups = lax.axis_size(FAR) * lax.axis_size(NEAR)
    picked = jnp.arange(groups) == member
    prompt = jnp.sum(jnp.where(picked, owner, 0))
    length = jnp.sum(jnp.where(picked, comp_len, 0))
    prompt_count = prefix_len.shape[0]
    prompt_ids = jnp.arange(prompt_count)
    offset = jnp.sum(jnp.where(prompt_ids < prompt, prefix_len, 0))
    span = jnp.sum(jnp.where(prompt_ids == prompt, prefix_len, 0))
    token_ids = jnp.arange(count)
    live = token_ids < length
    dout = jnp.where(live[:, None], out_grad[0], jnp.zeros_like(out_grad[0]))
    gathered = gather_prefix(prefix_kv[0])
    slots = gathered.shape[0]
    window = min(slots, 3 * slots // prompt_count)
    first = jnp.minimum(offset, slots - window)
    window_rows = lax.dynamic_slice_in_dim(gathered, first, window, 0)
    positions = first + jnp.arange(window)
    inside = (positions >= offset) & (positions < offset + span)
    causal = token_ids[:, None] >= token_ids[None, :]
    keys = jnp.concatenate([window_rows[:, :kv_width], own_keys], axis=0)
    values = jnp.concatenate([window_rows[:, kv_width:], own_values], axis=0)
    allowed = jnp.concatenate([jnp.broadcast_to(inside[None, :], (count, window)), causal], axis=1)
    total_keys = window + count
    q_four = queries.reshape(count, KV_HEADS, per, HEAD_DIM)
    d_four = dout.reshape(count, KV_HEADS, per, HEAD_DIM)
    v_three = values.reshape(total_keys, KV_HEADS, HEAD_DIM)
    scores = jnp.where(allowed[None, None], score_block(q_four, keys), jnp.float32(-1e30))
    top = jnp.max(scores, axis=-1, keepdims=True)
    expo = jnp.exp(scores - top)
    denom = jnp.sum(expo, axis=-1, keepdims=True)
    weights = expo / denom
    w_low = weights.astype(jnp.bfloat16)
    output = jnp.einsum("gqrm,mgh->gqrh", w_low, v_three, preferred_element_type=jnp.float32)
    delta = jnp.einsum("rgqh,gqrh->gqr", d_four.astype(jnp.float32), output)
    dprob = jnp.einsum("rgqh,mgh->gqrm", d_four, v_three, preferred_element_type=jnp.float32)
    d_low = (weights * (dprob - delta[..., None])).astype(jnp.bfloat16)
    k_three = keys.reshape(total_keys, KV_HEADS, HEAD_DIM)
    grad_q = jnp.einsum(
        "gqrm,mgh->rgqh", d_low, k_three, preferred_element_type=jnp.float32
    ) * HEAD_DIM ** (-0.5)
    grad_q = grad_q.reshape(count, width).astype(jnp.bfloat16)
    grad_pk, grad_pv = key_terms(d_low[..., :window], w_low[..., :window], q_four, d_four, window)
    window_term = jnp.concatenate([grad_pk, grad_pv], axis=1)
    full_term = lax.dynamic_update_slice_in_dim(
        jnp.zeros((slots, 2 * kv_width), jnp.float32), window_term, first, 0
    )
    near_sum, grad_q = lax.optimization_barrier((scatter_near(full_term), grad_q))
    passed = pass_down(grad_q[None], SECTION)
    prefix_grad = scatter_far(near_sum)
    passed, d_own, w_own = lax.optimization_barrier((passed, d_low[..., window:], w_low[..., window:]))
    grad_own_k, grad_own_v = key_terms(d_own, w_own, q_four, d_four, count)
    own_grad = jnp.concatenate([grad_own_k, grad_own_v], axis=1).astype(jnp.bfloat16)
    return (passed, own_grad[None], prefix_grad.astype(jnp.bfloat16)[None])


def solution(mesh):
    group_size = mesh.shape["group"]
    section_size = mesh.shape["section"]
    near_x, near_core = 4, 2
    layout = mesh.devices.reshape(
        group_size // (near_x * near_core), near_x, near_core, section_size // 4, 4
    )
    split = Mesh(layout, GROUP + SECTION)
    placed = P(SECTION, GROUP, None)
    in_specs = (placed, placed, placed, P(), P(), P())
    out_specs = (placed, placed, placed)
    return jax.shard_map(
        per_device, mesh=split, in_specs=in_specs, out_specs=out_specs, check_vma=False
    )
```

```python
import jax
import jax.numpy as jnp
from jax import lax
from jax.sharding import Mesh, PartitionSpec as P

HEADS = 16
KV_HEADS = 2
HEAD_DIM = 128

FAR = "group_z"
NEAR = ("group_x", "group_core")
GROUP = (FAR,) + NEAR
SECTION = ("section_y", "section_z")


def gather_prefix(block):
    far = lax.axis_size(FAR)
    near = lax.axis_size(NEAR)
    rows, width = block.shape
    spread = jnp.broadcast_to(block[None], (far, rows, width))
    column = lax.all_to_all(spread, FAR, 0, 0, tiled=True).reshape(far * rows, width)
    spread = jnp.broadcast_to(column[None], (near, far * rows, width))
    whole = lax.all_to_all(spread, NEAR, 0, 0, tiled=True)
    whole = whole.reshape(near, far, rows, width).transpose(1, 0, 2, 3)
    return whole.reshape(far * near * rows, width)


def scatter_sum(term):
    far = lax.axis_size(FAR)
    near = lax.axis_size(NEAR)
    slots, width = term.shape
    rows = slots // (far * near)
    parts = term.reshape(far, near, rows, width).transpose(1, 0, 2, 3)
    parts = parts.reshape(near, far * rows, width)
    parts = lax.all_to_all(parts, NEAR, 0, 0, tiled=True).sum(axis=0)
    parts = parts.reshape(far, rows, width)
    parts = lax.all_to_all(parts.astype(jnp.bfloat16), FAR, 0, 0, tiled=True)
    return parts.astype(jnp.float32).sum(axis=0)


def around(count, far_count, move):
    pairs = []
    for source in range(count):
        near, far = divmod(source, far_count)
        near, far = move(near, far)
        pairs.append((source, (near % (count // far_count)) * far_count + far % far_count))
    return pairs


def pass_down(value, axis):
    count = lax.axis_size(axis)
    far_count = lax.axis_size(axis[1])
    rows = value.shape[1]
    cut = rows - 3 * rows // 16
    direct = lax.ppermute(value[:, :cut], axis, around(count, far_count, lambda n, f: (n - (f == 0), f - 1)))
    rest = value[:, cut:]
    hop = around(count, far_count, lambda n, f: (n, f + 1))
    rest = lax.ppermute(rest, axis, hop)
    rest = lax.ppermute(rest, axis, hop)
    last = around(count, far_count, lambda n, f: (n - (f == 2), f + 1))
    rest = lax.ppermute(rest, axis, last)
    return jnp.concatenate([direct, rest], axis=1)


def from_behind(value, axis, steps):
    count = lax.axis_size(axis)
    pairs = [(source, (source + steps) % count) for source in range(count)]
    return lax.ppermute(value, axis, pairs)


def score_block(q_four, keys):
    total = keys.shape[0]
    k_three = keys.reshape(total, KV_HEADS, HEAD_DIM)
    return jnp.einsum(
        "rgqh,mgh->gqrm", q_four, k_three, preferred_element_type=jnp.float32
    ) * HEAD_DIM ** (-0.5)


def key_terms(d_low, w_low, q_four, d_four, total):
    grad_k = jnp.einsum(
        "gqrm,rgqh->mgh", d_low, q_four, preferred_element_type=jnp.float32
    ) * HEAD_DIM ** (-0.5)
    grad_v = jnp.einsum("gqrm,rgqh->mgh", w_low, d_four, preferred_element_type=jnp.float32)
    return (grad_k.reshape(total, KV_HEADS * HEAD_DIM), grad_v.reshape(total, KV_HEADS * HEAD_DIM))


def per_device(proj_rows, out_grad, prefix_kv, prefix_len, comp_len, owner):
    width = HEADS * HEAD_DIM
    kv_width = KV_HEADS * HEAD_DIM
    per = HEADS // KV_HEADS
    rows = proj_rows[0]
    count = rows.shape[0]
    queries = rows[:, :width]
    own_keys = rows[:, width : width + kv_width]
    own_values = rows[:, width + kv_width :]
    member = (lax.axis_index(FAR) * lax.axis_size(NEAR[0]) + lax.axis_index(NEAR[0])) * lax.axis_size(
        NEAR[1]
    ) + lax.axis_index(NEAR[1])
    groups = lax.axis_size(FAR) * lax.axis_size(NEAR)
    picked = jnp.arange(groups) == member
    prompt = jnp.sum(jnp.where(picked, owner, 0))
    length = jnp.sum(jnp.where(picked, comp_len, 0))
    prompt_count = prefix_len.shape[0]
    prompt_ids = jnp.arange(prompt_count)
    offset = jnp.sum(jnp.where(prompt_ids < prompt, prefix_len, 0))
    span = jnp.sum(jnp.where(prompt_ids == prompt, prefix_len, 0))
    token_ids = jnp.arange(count)
    live = token_ids < length
    dout = jnp.where(live[:, None], out_grad[0], jnp.zeros_like(out_grad[0]))
    gathered = gather_prefix(prefix_kv[0])
    slots = gathered.shape[0]
    window = min(slots, 3 * slots // prompt_count)
    first = jnp.minimum(offset, slots - window)
    window_rows = lax.dynamic_slice_in_dim(gathered, first, window, 0)
    positions = first + jnp.arange(window)
    inside = (positions >= offset) & (positions < offset + span)
    causal = token_ids[:, None] >= token_ids[None, :]
    keys = jnp.concatenate([window_rows[:, :kv_width], own_keys], axis=0)
    values = jnp.concatenate([window_rows[:, kv_width:], own_values], axis=0)
    allowed = jnp.concatenate([jnp.broadcast_to(inside[None, :], (count, window)), causal], axis=1)
    total_keys = window + count
    q_four = queries.reshape(count, KV_HEADS, per, HEAD_DIM)
    d_four = dout.reshape(count, KV_HEADS, per, HEAD_DIM)
    v_three = values.reshape(total_keys, KV_HEADS, HEAD_DIM)
    scores = jnp.where(allowed[None, None], score_block(q_four, keys), jnp.float32(-1e30))
    top = jnp.max(scores, axis=-1, keepdims=True)
    expo = jnp.exp(scores - top)
    denom = jnp.sum(expo, axis=-1, keepdims=True)
    weights = expo / denom
    w_low = weights.astype(jnp.bfloat16)
    output = jnp.einsum("gqrm,mgh->gqrh", w_low, v_three, preferred_element_type=jnp.float32)
    delta = jnp.einsum("rgqh,gqrh->gqr", d_four.astype(jnp.float32), output)
    dprob = jnp.einsum("rgqh,mgh->gqrm", d_four, v_three, preferred_element_type=jnp.float32)
    d_low = (weights * (dprob - delta[..., None])).astype(jnp.bfloat16)
    k_three = keys.reshape(total_keys, KV_HEADS, HEAD_DIM)
    grad_q = jnp.einsum(
        "gqrm,mgh->rgqh", d_low, k_three, preferred_element_type=jnp.float32
    ) * HEAD_DIM ** (-0.5)
    grad_q = grad_q.reshape(count, width).astype(jnp.bfloat16)
    passed = pass_down(grad_q[None], SECTION)
    grad_pk, grad_pv = key_terms(d_low[..., :window], w_low[..., :window], q_four, d_four, window)
    window_term = jnp.concatenate([grad_pk, grad_pv], axis=1)
    full_term = lax.dynamic_update_slice_in_dim(
        jnp.zeros((slots, 2 * kv_width), jnp.float32), window_term, first, 0
    )
    prefix_grad = scatter_sum(full_term)
    passed, d_own, w_own = lax.optimization_barrier((passed, d_low[..., window:], w_low[..., window:]))
    grad_own_k, grad_own_v = key_terms(d_own, w_own, q_four, d_four, count)
    own_grad = jnp.concatenate([grad_own_k, grad_own_v], axis=1).astype(jnp.bfloat16)
    return (passed, own_grad[None], prefix_grad.astype(jnp.bfloat16)[None])


def solution(mesh):
    group_size = mesh.shape["group"]
    section_size = mesh.shape["section"]
    near_x, near_core = 4, 2
    layout = mesh.devices.reshape(
        group_size // (near_x * near_core), near_x, near_core, section_size // 4, 4
    )
    split = Mesh(layout, GROUP + SECTION)
    placed = P(SECTION, GROUP, None)
    in_specs = (placed, placed, placed, P(), P(), P())
    out_specs = (placed, placed, placed)
    return jax.shard_map(
        per_device, mesh=split, in_specs=in_specs, out_specs=out_specs, check_vma=False
    )
```

```python
import jax
import jax.numpy as jnp
from jax import lax
from jax.sharding import Mesh, PartitionSpec as P

HEADS = 16
KV_HEADS = 2
HEAD_DIM = 128

FAR = "group_z"
NEAR = ("group_x", "group_core")
GROUP = (FAR,) + NEAR
SECTION = ("section_y", "section_z")


def gather_prefix(block):
    far = lax.axis_size(FAR)
    near = lax.axis_size(NEAR)
    rows, width = block.shape
    spread = jnp.broadcast_to(block[None], (far, rows, width))
    column = lax.all_to_all(spread, FAR, 0, 0, tiled=True).reshape(far * rows, width)
    spread = jnp.broadcast_to(column[None], (near, far * rows, width))
    whole = lax.all_to_all(spread, NEAR, 0, 0, tiled=True)
    whole = whole.reshape(near, far, rows, width).transpose(1, 0, 2, 3)
    return whole.reshape(far * near * rows, width)


def scatter_sum(term):
    far = lax.axis_size(FAR)
    near = lax.axis_size(NEAR)
    slots, width = term.shape
    rows = slots // (far * near)
    parts = term.reshape(far, near, rows, width).transpose(1, 0, 2, 3)
    parts = parts.reshape(near, far * rows, width)
    parts = lax.all_to_all(parts, NEAR, 0, 0, tiled=True).sum(axis=0)
    parts = parts.reshape(far, rows, width)
    return lax.all_to_all(parts, FAR, 0, 0, tiled=True).sum(axis=0)


def around(count, far_count, move):
    pairs = []
    for source in range(count):
        near, far = divmod(source, far_count)
        near, far = move(near, far)
        pairs.append((source, (near % (count // far_count)) * far_count + far % far_count))
    return pairs


def pass_down(value, axis):
    count = lax.axis_size(axis)
    far_count = lax.axis_size(axis[1])
    rows = value.shape[1]
    cut = rows - 3 * rows // 16
    direct = lax.ppermute(value[:, :cut], axis, around(count, far_count, lambda n, f: (n - (f == 0), f - 1)))
    rest = value[:, cut:]
    hop = around(count, far_count, lambda n, f: (n, f + 1))
    rest = lax.ppermute(rest, axis, hop)
    rest = lax.ppermute(rest, axis, hop)
    last = around(count, far_count, lambda n, f: (n - (f == 2), f + 1))
    rest = lax.ppermute(rest, axis, last)
    return jnp.concatenate([direct, rest], axis=1)


def from_behind(value, axis, steps):
    count = lax.axis_size(axis)
    pairs = [(source, (source + steps) % count) for source in range(count)]
    return lax.ppermute(value, axis, pairs)


def score_block(q_four, keys):
    total = keys.shape[0]
    k_three = keys.reshape(total, KV_HEADS, HEAD_DIM)
    return jnp.einsum(
        "rgqh,mgh->gqrm", q_four, k_three, preferred_element_type=jnp.float32
    ) * HEAD_DIM ** (-0.5)


def key_terms(d_low, w_low, q_four, d_four, total):
    grad_k = jnp.einsum(
        "gqrm,rgqh->mgh", d_low, q_four, preferred_element_type=jnp.float32
    ) * HEAD_DIM ** (-0.5)
    grad_v = jnp.einsum("gqrm,rgqh->mgh", w_low, d_four, preferred_element_type=jnp.float32)
    return (grad_k.reshape(total, KV_HEADS * HEAD_DIM), grad_v.reshape(total, KV_HEADS * HEAD_DIM))


def per_device(proj_rows, out_grad, prefix_kv, prefix_len, comp_len, owner):
    width = HEADS * HEAD_DIM
    kv_width = KV_HEADS * HEAD_DIM
    per = HEADS // KV_HEADS
    rows = proj_rows[0]
    count = rows.shape[0]
    queries = rows[:, :width]
    own_keys = rows[:, width : width + kv_width]
    own_values = rows[:, width + kv_width :]
    member = (lax.axis_index(FAR) * lax.axis_size(NEAR[0]) + lax.axis_index(NEAR[0])) * lax.axis_size(
        NEAR[1]
    ) + lax.axis_index(NEAR[1])
    groups = lax.axis_size(FAR) * lax.axis_size(NEAR)
    picked = jnp.arange(groups) == member
    prompt = jnp.sum(jnp.where(picked, owner, 0))
    length = jnp.sum(jnp.where(picked, comp_len, 0))
    prompt_count = prefix_len.shape[0]
    prompt_ids = jnp.arange(prompt_count)
    offset = jnp.sum(jnp.where(prompt_ids < prompt, prefix_len, 0))
    span = jnp.sum(jnp.where(prompt_ids == prompt, prefix_len, 0))
    token_ids = jnp.arange(count)
    live = token_ids < length
    dout = jnp.where(live[:, None], out_grad[0], jnp.zeros_like(out_grad[0]))
    gathered = gather_prefix(prefix_kv[0])
    slots = gathered.shape[0]
    window = min(slots, 3 * slots // prompt_count)
    first = jnp.minimum(offset, slots - window)
    window_rows = lax.dynamic_slice_in_dim(gathered, first, window, 0)
    positions = first + jnp.arange(window)
    inside = (positions >= offset) & (positions < offset + span)
    causal = token_ids[:, None] >= token_ids[None, :]
    keys = jnp.concatenate([window_rows[:, :kv_width], own_keys], axis=0)
    values = jnp.concatenate([window_rows[:, kv_width:], own_values], axis=0)
    allowed = jnp.concatenate([jnp.broadcast_to(inside[None, :], (count, window)), causal], axis=1)
    total_keys = window + count
    q_four = queries.reshape(count, KV_HEADS, per, HEAD_DIM)
    d_four = dout.reshape(count, KV_HEADS, per, HEAD_DIM)
    v_three = values.reshape(total_keys, KV_HEADS, HEAD_DIM)
    raw = jnp.concatenate(
        [score_block(q_four, window_rows[:, :kv_width]), score_block(q_four, own_keys)], axis=-1
    )
    scores = jnp.where(allowed[None, None], raw, jnp.float32(-1e30))
    top = jnp.max(scores, axis=-1, keepdims=True)
    expo = jnp.exp(scores - top)
    denom = jnp.sum(expo, axis=-1, keepdims=True)
    weights = expo / denom
    w_low = weights.astype(jnp.bfloat16)
    output = jnp.einsum("gqrm,mgh->gqrh", w_low, v_three, preferred_element_type=jnp.float32)
    delta = jnp.einsum("rgqh,gqrh->gqr", d_four.astype(jnp.float32), output)
    v_window = window_rows[:, kv_width:].reshape(window, KV_HEADS, HEAD_DIM)
    v_own = own_values.reshape(count, KV_HEADS, HEAD_DIM)
    dprob = jnp.concatenate(
        [
            jnp.einsum("rgqh,mgh->gqrm", d_four, v_window, preferred_element_type=jnp.float32),
            jnp.einsum("rgqh,mgh->gqrm", d_four, v_own, preferred_element_type=jnp.float32),
        ],
        axis=-1,
    )
    d_low = (weights * (dprob - delta[..., None])).astype(jnp.bfloat16)
    k_three = keys.reshape(total_keys, KV_HEADS, HEAD_DIM)
    grad_q = jnp.einsum(
        "gqrm,mgh->rgqh", d_low, k_three, preferred_element_type=jnp.float32
    ) * HEAD_DIM ** (-0.5)
    grad_q = grad_q.reshape(count, width).astype(jnp.bfloat16)
    passed = pass_down(grad_q[None], SECTION)
    grad_pk, grad_pv = key_terms(d_low[..., :window], w_low[..., :window], q_four, d_four, window)
    window_term = jnp.concatenate([grad_pk, grad_pv], axis=1)
    full_term = lax.dynamic_update_slice_in_dim(
        jnp.zeros((slots, 2 * kv_width), jnp.float32), window_term, first, 0
    )
    prefix_grad = scatter_sum(full_term)
    passed, d_own, w_own = lax.optimization_barrier((passed, d_low[..., window:], w_low[..., window:]))
    grad_own_k, grad_own_v = key_terms(d_own, w_own, q_four, d_four, count)
    own_grad = jnp.concatenate([grad_own_k, grad_own_v], axis=1).astype(jnp.bfloat16)
    return (passed, own_grad[None], prefix_grad.astype(jnp.bfloat16)[None])


def solution(mesh):
    group_size = mesh.shape["group"]
    section_size = mesh.shape["section"]
    near_x, near_core = 4, 2
    layout = mesh.devices.reshape(
        group_size // (near_x * near_core), near_x, near_core, section_size // 4, 4
    )
    split = Mesh(layout, GROUP + SECTION)
    placed = P(SECTION, GROUP, None)
    in_specs = (placed, placed, placed, P(), P(), P())
    out_specs = (placed, placed, placed)
    return jax.shard_map(
        per_device, mesh=split, in_specs=in_specs, out_specs=out_specs, check_vma=False
    )
```

```python
import jax
import jax.numpy as jnp
from jax import lax
from jax.sharding import Mesh, PartitionSpec as P

HEADS = 16
KV_HEADS = 2
HEAD_DIM = 128

FAR = "group_z"
NEAR = ("group_x", "group_core")
GROUP = (FAR,) + NEAR
SECTION = ("section_y", "section_z")


def gather_prefix(block):
    far = lax.axis_size(FAR)
    near = lax.axis_size(NEAR)
    rows, width = block.shape
    spread = jnp.broadcast_to(block[None], (far, rows, width))
    column = lax.all_to_all(spread, FAR, 0, 0, tiled=True).reshape(far * rows, width)
    spread = jnp.broadcast_to(column[None], (near, far * rows, width))
    whole = lax.all_to_all(spread, NEAR, 0, 0, tiled=True)
    whole = whole.reshape(near, far, rows, width).transpose(1, 0, 2, 3)
    return whole.reshape(far * near * rows, width)


def scatter_sum(term):
    far = lax.axis_size(FAR)
    near = lax.axis_size(NEAR)
    slots, width = term.shape
    rows = slots // (far * near)
    parts = term.reshape(far, near, rows, width).transpose(1, 0, 2, 3)
    parts = parts.reshape(near, far * rows, width)
    parts = lax.all_to_all(parts, NEAR, 0, 0, tiled=True).sum(axis=0)
    parts = parts.reshape(far, rows, width)
    return lax.all_to_all(parts, FAR, 0, 0, tiled=True).sum(axis=0)


def around(count, far_count, move):
    pairs = []
    for source in range(count):
        near, far = divmod(source, far_count)
        near, far = move(near, far)
        pairs.append((source, (near % (count // far_count)) * far_count + far % far_count))
    return pairs


def pass_down(value, axis):
    count = lax.axis_size(axis)
    far_count = lax.axis_size(axis[1])
    rows = value.shape[1]
    cut = rows - rows // 4
    direct = lax.ppermute(value[:, :cut], axis, around(count, far_count, lambda n, f: (n - (f == 0), f - 1)))
    rest = value[:, cut:]
    hop = around(count, far_count, lambda n, f: (n, f + 1))
    rest = lax.ppermute(rest, axis, hop)
    rest = lax.ppermute(rest, axis, hop)
    last = around(count, far_count, lambda n, f: (n - (f == 2), f + 1))
    rest = lax.ppermute(rest, axis, last)
    return jnp.concatenate([direct, rest], axis=1)


def from_behind(value, axis, steps):
    count = lax.axis_size(axis)
    pairs = [(source, (source + steps) % count) for source in range(count)]
    return lax.ppermute(value, axis, pairs)


def score_block(q_four, keys):
    total = keys.shape[0]
    k_three = keys.reshape(total, KV_HEADS, HEAD_DIM)
    return jnp.einsum(
        "rgqh,mgh->gqrm", q_four, k_three, preferred_element_type=jnp.float32
    ) * HEAD_DIM ** (-0.5)


def key_terms(d_low, w_low, q_four, d_four, total):
    grad_k = jnp.einsum(
        "gqrm,rgqh->mgh", d_low, q_four, preferred_element_type=jnp.float32
    ) * HEAD_DIM ** (-0.5)
    grad_v = jnp.einsum("gqrm,rgqh->mgh", w_low, d_four, preferred_element_type=jnp.float32)
    return (grad_k.reshape(total, KV_HEADS * HEAD_DIM), grad_v.reshape(total, KV_HEADS * HEAD_DIM))


def per_device(proj_rows, out_grad, prefix_kv, prefix_len, comp_len, owner):
    width = HEADS * HEAD_DIM
    kv_width = KV_HEADS * HEAD_DIM
    per = HEADS // KV_HEADS
    rows = proj_rows[0]
    count = rows.shape[0]
    queries = rows[:, :width]
    own_keys = rows[:, width : width + kv_width]
    own_values = rows[:, width + kv_width :]
    member = (lax.axis_index(FAR) * lax.axis_size(NEAR[0]) + lax.axis_index(NEAR[0])) * lax.axis_size(
        NEAR[1]
    ) + lax.axis_index(NEAR[1])
    groups = lax.axis_size(FAR) * lax.axis_size(NEAR)
    picked = jnp.arange(groups) == member
    prompt = jnp.sum(jnp.where(picked, owner, 0))
    length = jnp.sum(jnp.where(picked, comp_len, 0))
    prompt_count = prefix_len.shape[0]
    prompt_ids = jnp.arange(prompt_count)
    offset = jnp.sum(jnp.where(prompt_ids < prompt, prefix_len, 0))
    span = jnp.sum(jnp.where(prompt_ids == prompt, prefix_len, 0))
    token_ids = jnp.arange(count)
    live = token_ids < length
    dout = jnp.where(live[:, None], out_grad[0], jnp.zeros_like(out_grad[0]))
    gathered = gather_prefix(prefix_kv[0])
    slots = gathered.shape[0]
    window = min(slots, 3 * slots // prompt_count)
    first = jnp.minimum(offset, slots - window)
    window_rows = lax.dynamic_slice_in_dim(gathered, first, window, 0)
    positions = first + jnp.arange(window)
    inside = (positions >= offset) & (positions < offset + span)
    causal = token_ids[:, None] >= token_ids[None, :]
    keys = jnp.concatenate([window_rows[:, :kv_width], own_keys], axis=0)
    values = jnp.concatenate([window_rows[:, kv_width:], own_values], axis=0)
    allowed = jnp.concatenate([jnp.broadcast_to(inside[None, :], (count, window)), causal], axis=1)
    total_keys = window + count
    q_four = queries.reshape(count, KV_HEADS, per, HEAD_DIM)
    d_four = dout.reshape(count, KV_HEADS, per, HEAD_DIM)
    v_three = values.reshape(total_keys, KV_HEADS, HEAD_DIM)
    scores = jnp.where(allowed[None, None], score_block(q_four, keys), jnp.float32(-1e30))
    top = jnp.max(scores, axis=-1, keepdims=True)
    expo = jnp.exp(scores - top)
    denom = jnp.sum(expo, axis=-1, keepdims=True)
    weights = expo / denom
    w_low = weights.astype(jnp.bfloat16)
    output = jnp.einsum("gqrm,mgh->gqrh", w_low, v_three, preferred_element_type=jnp.float32)
    delta = jnp.einsum("rgqh,gqrh->gqr", d_four.astype(jnp.float32), output)
    dprob = jnp.einsum("rgqh,mgh->gqrm", d_four, v_three, preferred_element_type=jnp.float32)
    d_low = (weights * (dprob - delta[..., None])).astype(jnp.bfloat16)
    k_three = keys.reshape(total_keys, KV_HEADS, HEAD_DIM)
    grad_q = jnp.einsum(
        "gqrm,mgh->rgqh", d_low, k_three, preferred_element_type=jnp.float32
    ) * HEAD_DIM ** (-0.5)
    grad_q = grad_q.reshape(count, width).astype(jnp.bfloat16)
    passed = pass_down(grad_q[None], SECTION)
    grad_pk, grad_pv = key_terms(d_low[..., :window], w_low[..., :window], q_four, d_four, window)
    window_term = jnp.concatenate([grad_pk, grad_pv], axis=1)
    full_term = lax.dynamic_update_slice_in_dim(
        jnp.zeros((slots, 2 * kv_width), jnp.float32), window_term, first, 0
    )
    prefix_grad = scatter_sum(full_term)
    passed, d_own, w_own = lax.optimization_barrier((passed, d_low[..., window:], w_low[..., window:]))
    grad_own_k, grad_own_v = key_terms(d_own, w_own, q_four, d_four, count)
    own_grad = jnp.concatenate([grad_own_k, grad_own_v], axis=1).astype(jnp.bfloat16)
    return (passed, own_grad[None], prefix_grad.astype(jnp.bfloat16)[None])


def solution(mesh):
    group_size = mesh.shape["group"]
    section_size = mesh.shape["section"]
    near_x, near_core = 4, 2
    layout = mesh.devices.reshape(
        group_size // (near_x * near_core), near_x, near_core, section_size // 4, 4
    )
    split = Mesh(layout, GROUP + SECTION)
    placed = P(SECTION, GROUP, None)
    in_specs = (placed, placed, placed, P(), P(), P())
    out_specs = (placed, placed, placed)
    return jax.shard_map(
        per_device, mesh=split, in_specs=in_specs, out_specs=out_specs, check_vma=False
    )
```

```python
import jax
import jax.numpy as jnp
from jax import lax
from jax.sharding import Mesh, PartitionSpec as P

HEADS = 16
KV_HEADS = 2
HEAD_DIM = 128

FAR = "group_z"
NEAR = ("group_x", "group_core")
GROUP = (FAR,) + NEAR
SECTION = ("section_y", "section_z")


def gather_prefix(block):
    far = lax.axis_size(FAR)
    near = lax.axis_size(NEAR)
    rows, width = block.shape
    spread = jnp.broadcast_to(block[None], (far, rows, width))
    column = lax.all_to_all(spread, FAR, 0, 0, tiled=True).reshape(far * rows, width)
    spread = jnp.broadcast_to(column[None], (near, far * rows, width))
    whole = lax.all_to_all(spread, NEAR, 0, 0, tiled=True)
    whole = whole.reshape(near, far, rows, width).transpose(1, 0, 2, 3)
    return whole.reshape(far * near * rows, width)


def scatter_sum(term):
    far = lax.axis_size(FAR)
    near = lax.axis_size(NEAR)
    slots, width = term.shape
    rows = slots // (far * near)
    parts = term.reshape(far, near, rows, width).transpose(1, 0, 2, 3)
    parts = parts.reshape(near, far * rows, width)
    parts = lax.all_to_all(parts, NEAR, 0, 0, tiled=True).sum(axis=0)
    parts = parts.reshape(far, rows, width)
    return lax.all_to_all(parts, FAR, 0, 0, tiled=True).sum(axis=0)


def around(count, far_count, move):
    pairs = []
    for source in range(count):
        near, far = divmod(source, far_count)
        near, far = move(near, far)
        pairs.append((source, (near % (count // far_count)) * far_count + far % far_count))
    return pairs


def pass_down(value, axis):
    count = lax.axis_size(axis)
    far_count = lax.axis_size(axis[1])
    rows = value.shape[1]
    cut = rows - 7 * rows // 32
    direct = lax.ppermute(value[:, :cut], axis, around(count, far_count, lambda n, f: (n - (f == 0), f - 1)))
    rest = value[:, cut:]
    hop = around(count, far_count, lambda n, f: (n, f + 1))
    rest = lax.ppermute(rest, axis, hop)
    rest = lax.ppermute(rest, axis, hop)
    last = around(count, far_count, lambda n, f: (n - (f == 2), f + 1))
    rest = lax.ppermute(rest, axis, last)
    return jnp.concatenate([direct, rest], axis=1)


def from_behind(value, axis, steps):
    count = lax.axis_size(axis)
    pairs = [(source, (source + steps) % count) for source in range(count)]
    return lax.ppermute(value, axis, pairs)


def score_block(q_four, keys):
    total = keys.shape[0]
    k_three = keys.reshape(total, KV_HEADS, HEAD_DIM)
    return jnp.einsum(
        "rgqh,mgh->gqrm", q_four, k_three, preferred_element_type=jnp.float32
    ) * HEAD_DIM ** (-0.5)


def key_terms(d_low, w_low, q_four, d_four, total):
    grad_k = jnp.einsum(
        "gqrm,rgqh->mgh", d_low, q_four, preferred_element_type=jnp.float32
    ) * HEAD_DIM ** (-0.5)
    grad_v = jnp.einsum("gqrm,rgqh->mgh", w_low, d_four, preferred_element_type=jnp.float32)
    return (grad_k.reshape(total, KV_HEADS * HEAD_DIM), grad_v.reshape(total, KV_HEADS * HEAD_DIM))


def per_device(proj_rows, out_grad, prefix_kv, prefix_len, comp_len, owner):
    width = HEADS * HEAD_DIM
    kv_width = KV_HEADS * HEAD_DIM
    per = HEADS // KV_HEADS
    rows = proj_rows[0]
    count = rows.shape[0]
    queries = rows[:, :width]
    own_keys = rows[:, width : width + kv_width]
    own_values = rows[:, width + kv_width :]
    member = (lax.axis_index(FAR) * lax.axis_size(NEAR[0]) + lax.axis_index(NEAR[0])) * lax.axis_size(
        NEAR[1]
    ) + lax.axis_index(NEAR[1])
    groups = lax.axis_size(FAR) * lax.axis_size(NEAR)
    picked = jnp.arange(groups) == member
    prompt = jnp.sum(jnp.where(picked, owner, 0))
    length = jnp.sum(jnp.where(picked, comp_len, 0))
    prompt_count = prefix_len.shape[0]
    prompt_ids = jnp.arange(prompt_count)
    offset = jnp.sum(jnp.where(prompt_ids < prompt, prefix_len, 0))
    span = jnp.sum(jnp.where(prompt_ids == prompt, prefix_len, 0))
    token_ids = jnp.arange(count)
    live = token_ids < length
    dout = jnp.where(live[:, None], out_grad[0], jnp.zeros_like(out_grad[0]))
    gathered = gather_prefix(prefix_kv[0])
    slots = gathered.shape[0]
    window = min(slots, 3 * slots // prompt_count)
    first = jnp.minimum(offset, slots - window)
    window_rows = lax.dynamic_slice_in_dim(gathered, first, window, 0)
    positions = first + jnp.arange(window)
    inside = (positions >= offset) & (positions < offset + span)
    causal = token_ids[:, None] >= token_ids[None, :]
    keys = jnp.concatenate([window_rows[:, :kv_width], own_keys], axis=0)
    values = jnp.concatenate([window_rows[:, kv_width:], own_values], axis=0)
    allowed = jnp.concatenate([jnp.broadcast_to(inside[None, :], (count, window)), causal], axis=1)
    total_keys = window + count
    q_four = queries.reshape(count, KV_HEADS, per, HEAD_DIM)
    d_four = dout.reshape(count, KV_HEADS, per, HEAD_DIM)
    v_three = values.reshape(total_keys, KV_HEADS, HEAD_DIM)
    scores = jnp.where(allowed[None, None], score_block(q_four, keys), jnp.float32(-1e30))
    top = jnp.max(scores, axis=-1, keepdims=True)
    expo = jnp.exp(scores - top)
    denom = jnp.sum(expo, axis=-1, keepdims=True)
    weights = expo / denom
    w_low = weights.astype(jnp.bfloat16)
    output = jnp.einsum("gqrm,mgh->gqrh", w_low, v_three, preferred_element_type=jnp.float32)
    delta = jnp.einsum("rgqh,gqrh->gqr", d_four.astype(jnp.float32), output)
    dprob = jnp.einsum("rgqh,mgh->gqrm", d_four, v_three, preferred_element_type=jnp.float32)
    d_low = (weights * (dprob - delta[..., None])).astype(jnp.bfloat16)
    k_three = keys.reshape(total_keys, KV_HEADS, HEAD_DIM)
    grad_q = jnp.einsum(
        "gqrm,mgh->rgqh", d_low, k_three, preferred_element_type=jnp.float32
    ) * HEAD_DIM ** (-0.5)
    grad_q = grad_q.reshape(count, width).astype(jnp.bfloat16)
    passed = pass_down(grad_q[None], SECTION)
    grad_pk, grad_pv = key_terms(d_low[..., :window], w_low[..., :window], q_four, d_four, window)
    window_term = jnp.concatenate([grad_pk, grad_pv], axis=1)
    full_term = lax.dynamic_update_slice_in_dim(
        jnp.zeros((slots, 2 * kv_width), jnp.float32), window_term, first, 0
    )
    prefix_grad = scatter_sum(full_term)
    passed, d_own, w_own = lax.optimization_barrier((passed, d_low[..., window:], w_low[..., window:]))
    grad_own_k, grad_own_v = key_terms(d_own, w_own, q_four, d_four, count)
    own_grad = jnp.concatenate([grad_own_k, grad_own_v], axis=1).astype(jnp.bfloat16)
    return (passed, own_grad[None], prefix_grad.astype(jnp.bfloat16)[None])


def solution(mesh):
    group_size = mesh.shape["group"]
    section_size = mesh.shape["section"]
    near_x, near_core = 4, 2
    layout = mesh.devices.reshape(
        group_size // (near_x * near_core), near_x, near_core, section_size // 4, 4
    )
    split = Mesh(layout, GROUP + SECTION)
    placed = P(SECTION, GROUP, None)
    in_specs = (placed, placed, placed, P(), P(), P())
    out_specs = (placed, placed, placed)
    return jax.shard_map(
        per_device, mesh=split, in_specs=in_specs, out_specs=out_specs, check_vma=False
    )
```
